32 devices in a mesh: groups: 2 (over y), prompt: 4 (over x, core), resp: 4 (over z).
Axes of the slice: x: 2, y: 2, z: 4, core: 2. Of those that a mesh axis runs over, the one named last changes fastest.
Arguments:
- queries: bfloat16 [8, 4, 32, 8192], P(('groups', 'prompt'), 'resp'), parts along dimension 0, may hold values from -90 to 90
- cotangent: bfloat16 [8, 4, 32, 8192], P(('groups', 'prompt'), 'resp'), parts along dimension 0, may hold values from -6 to 6
- resp_keys: bfloat16 [8, 4, 32, 512], P(('groups', 'prompt'), 'resp'), parts along dimension 0, may hold values from -6 to 6
- resp_values: bfloat16 [8, 4, 32, 512], P(('groups', 'prompt'), 'resp'), parts along dimension 0, may hold values from -6 to 6
- prefix_keys: bfloat16 [8, 512, 512], P(('groups', 'prompt'), 'resp'), parts along dimension 0, may hold values from -5 to 5
- prefix_values: bfloat16 [8, 512, 512], P(('groups', 'prompt'), 'resp'), parts along dimension 0, may hold values from -6 to 6
- counts: int32 [8], P(('groups', 'prompt')), parts along dimension 0, may hold values from 1 to 4, as said below
- lengths: int32 [8, 4], P(('groups', 'prompt'), 'resp'), parts along dimension 0, may hold values from 8 to 32, as said below
- policy_likelihood: float32 [8, 4], P(('groups', 'prompt'), 'resp'), parts along dimension 0, may hold values from -8 to 8
- reference_likelihood: float32 [8, 4], P(('groups', 'prompt'), 'resp'), parts along dimension 0, may hold values from -8 to 8
Outputs:
- grad_queries: bfloat16 [8, 4, 32, 8192], P(('groups', 'prompt'), 'resp'), parts along dimension 0
- grad_resp_keys: bfloat16 [8, 4, 32, 512], P(('groups', 'prompt'), 'resp'), parts along dimension 0
- grad_resp_values: bfloat16 [8, 4, 32, 512], P(('groups', 'prompt'), 'resp'), parts along dimension 0
- grad_prefix_keys: bfloat16 [8, 512, 512], P(('groups', 'prompt'), 'resp'), parts along dimension 0
- grad_prefix_values: bfloat16 [8, 512, 512], P(('groups', 'prompt'), 'resp'), parts along dimension 0
- forget_loss: float32 [8], P(('groups', 'prompt')), parts along dimension 0
The draws below stay inside these ranges and needn't reach their ends.
There are 2 independent parts, one for each index of `groups`. The reference program is written for one: setup_inputs(seed, part) draws one part's arguments, and reference() takes and returns one part's arrays. A program takes and returns all parts, laid end to end along the dimension named above; each array names one. Nothing has to cross between parts.
Inputs may be any that keep to these rules, and one draw needn't show every extreme that they name: `counts`: live responses of a prompt fill its first slots; some prompt has all 4. `lengths`: tokens of a response are its first slots, the rest padding; each prompt has a live response of 32 tokens.
All inputs are finite; a program needn't handle non-finite values.
Results may differ from the reference program's by a relative error of at most 0.0085.
Values may be sent and summed in bfloat16 or wider, within the bound.
No kernel may reach another device: no remote copies, remote signals or barrier semaphores. Data moves between devices by JAX's collectives and lax.ppermute only.
A program may use at most 128 MiB of HBM per device.

```python
import math
import jax
import jax.numpy as jnp
from jax import lax

HEADS = 64
KV_HEADS = 4
HEAD_DIM = 128
RL = 32
RESP_DEV = 1
PROMPTS = 4
SLOTS = 4
LP = 512
N_RESP = 4


def prompt_counts(key):
    inner = jax.random.fold_in(key, 11)
    first_key, second_key = jax.random.split(inner)
    drawn = jax.random.randint(first_key, (PROMPTS,), 1, SLOTS + 1)
    fullest = jax.random.randint(second_key, (), 0, PROMPTS)
    return jnp.where(jnp.arange(PROMPTS) == fullest, SLOTS, drawn).astype(jnp.int32)


def draw_counts(key, part):
    return prompt_counts(key)


def draw_lengths(key, part):
    live_counts = prompt_counts(key)
    inner = jax.random.fold_in(key, 23)
    first_key, second_key = jax.random.split(inner)
    drawn = jax.random.randint(first_key, (PROMPTS, SLOTS), max(1, RL // 4), RL + 1)
    longest = jax.random.randint(second_key, (PROMPTS,), 0, live_counts)
    slot_ids = jnp.arange(SLOTS)[None, :]
    return jnp.where(slot_ids == longest[:, None], RL, drawn).astype(jnp.int32)


def prefix_draw(key):
    inner = jax.random.fold_in(key, 37)
    first_key = jax.random.fold_in(inner, 0)
    base = jnp.clip(jax.random.normal(first_key, (PROMPTS, LP, KV_HEADS * HEAD_DIM), jnp.float32), -4.5, 4.5)
    return base


def draw_prefix_keys(key, part):
    return prefix_draw(key).astype(jnp.bfloat16)


def draw_queries(key, part):
    inner = jax.random.fold_in(key, 53)
    shape = (PROMPTS, SLOTS, RL, HEADS * HEAD_DIM)
    values_out = jnp.clip(jax.random.normal(inner, shape, jnp.float32), -5.0, 5.0)
    return values_out.astype(jnp.bfloat16)


def block_scale(stream_key, extent, shards, smallest, high):
    def one(position, blocks):
        heights = jax.random.uniform(jax.random.fold_in(jax.random.fold_in(stream_key, 6), position), (blocks,), jnp.float32, smallest / len(shards), high / len(shards))
        return jnp.repeat(jnp.exp(heights), extent[position] // blocks).reshape((-1,) + (1,) * (len(extent) - position - 1))

    factor_of = one(*shards[0])
    for cut in shards[1:]:
        factor_of = factor_of * one(*cut)
    return factor_of


def normal_values(key, extent, width, reach, shards=(), kind=jnp.bfloat16):
    array = jax.random.normal(key, extent, jnp.float32) * width
    if len(shards) > 0:
        array = block_scale(key, extent, shards, -0.22, 0.18) * array
    return jnp.clip(array, min=-reach, max=reach).astype(kind)


def setup_inputs(seed: int = 0, part: int = 0) -> dict:
    key_list = jax.random.split(jax.random.key(seed), 11)
    part_keys = jax.random.split(jax.random.fold_in(key_list[10], part), 11)
    queries = draw_queries(jax.random.fold_in(jax.random.fold_in(key_list[10], part), 71), part)
    cotangent = normal_values(part_keys[1], (PROMPTS, SLOTS, RL, HEADS * HEAD_DIM), 1.0, 6.0, ((0, 4), (1, 4)))
    resp_keys = normal_values(part_keys[2], (PROMPTS, SLOTS, RL, KV_HEADS * HEAD_DIM), 1.0, 6.0, ((0, 4), (1, 4)))
    resp_values = normal_values(part_keys[3], (PROMPTS, SLOTS, RL, KV_HEADS * HEAD_DIM), 1.0, 6.0, ((0, 4), (1, 4)))
    prefix_keys = draw_prefix_keys(jax.random.fold_in(jax.random.fold_in(key_list[10], part), 71), part)
    prefix_values = normal_values(part_keys[5], (PROMPTS, LP, KV_HEADS * HEAD_DIM), 1.0, 6.0, ((0, 4), (1, 4)))
    counts = draw_counts(jax.random.fold_in(jax.random.fold_in(key_list[10], part), 71), part)
    lengths = draw_lengths(jax.random.fold_in(jax.random.fold_in(key_list[10], part), 71), part)
    policy_likelihood = normal_values(part_keys[8], (PROMPTS, SLOTS), 2.0, 8.0, ((0, 4), (1, 4)), jnp.float32)
    reference_likelihood = normal_values(part_keys[9], (PROMPTS, SLOTS), 2.0, 8.0, ((0, 4), (1, 4)), jnp.float32)
    return dict(queries=queries, cotangent=cotangent, resp_keys=resp_keys, resp_values=resp_values, prefix_keys=prefix_keys, prefix_values=prefix_values, counts=counts, lengths=lengths, policy_likelihood=policy_likelihood, reference_likelihood=reference_likelihood)


loss_beta = 0.5
masked_score = -1e+30

def block_sum(left_rows, right_rows, scaling):
    rows_per = RESP_DEV * RL * (HEADS // KV_HEADS)
    left_dev = left_rows.reshape(N_RESP, rows_per, left_rows.shape[1]).astype(jnp.float32)
    right_dev = right_rows.reshape(N_RESP, rows_per, right_rows.shape[1]).astype(jnp.float32)
    parts = jnp.einsum('nrj,nrd->njd', left_dev, right_dev) * scaling
    rounded = lax.optimization_barrier(parts.astype(jnp.bfloat16))
    return lax.optimization_barrier(jnp.sum(rounded.astype(jnp.float32), axis=0))

def prompt_terms(packed):
    queries, cotangent, resp_keys, resp_values, prefix_keys, prefix_values, live_count, lengths, policy_likelihood, reference_likelihood = packed
    group_size = HEADS // KV_HEADS
    group_width = group_size * HEAD_DIM
    scaling = 1.0 / math.sqrt(HEAD_DIM)
    count_real = live_count.astype(jnp.float32)
    slot_ids = jnp.arange(SLOTS, dtype=jnp.int32)
    live_slots = slot_ids < live_count
    margin = policy_likelihood - reference_likelihood
    weight = jnp.where(live_slots, 2.0 * jax.nn.sigmoid(loss_beta * margin) / count_real, 0.0)
    loss_terms = jnp.where(live_slots, 2.0 / loss_beta * jax.nn.softplus(loss_beta * margin), 0.0)
    forget_loss = jnp.sum(loss_terms) / count_real
    positions = jnp.arange(RL, dtype=jnp.int32)
    kept_tokens = positions[None, :] < lengths[:, None]
    factor = jnp.where(kept_tokens, weight[:, None], 0.0)
    grad_out = (cotangent.astype(jnp.float32) * factor[:, :, None]).astype(jnp.bfloat16)
    causal = positions[:, None] >= positions[None, :]
    query_grads, key_grads, value_grads, prefix_key_parts, prefix_value_parts = ([], [], [], [], [])
    for group_index in range(KV_HEADS):
        low = group_index * group_width
        query_four = queries[:, :, low:low + group_width].reshape(SLOTS, RL, group_size, HEAD_DIM)
        grad_four = grad_out[:, :, low:low + group_width].reshape(SLOTS, RL, group_size, HEAD_DIM)
        own_keys = resp_keys[:, :, group_index * HEAD_DIM:(group_index + 1) * HEAD_DIM]
        own_values = resp_values[:, :, group_index * HEAD_DIM:(group_index + 1) * HEAD_DIM]
        head_keys = prefix_keys[:, group_index * HEAD_DIM:(group_index + 1) * HEAD_DIM]
        head_values = prefix_values[:, group_index * HEAD_DIM:(group_index + 1) * HEAD_DIM]
        query_rows = query_four.reshape(-1, HEAD_DIM)
        grad_rows = grad_four.reshape(-1, HEAD_DIM)
        scores_pre = jnp.dot(query_rows, head_keys.T, preferred_element_type=jnp.float32) * scaling
        scores_own = jnp.einsum('sqgd,skd->sqgk', query_four.astype(jnp.float32), own_keys.astype(jnp.float32)) * scaling
        scores_own = jnp.where(causal[None, :, None, :], scores_own, masked_score).reshape(-1, RL)
        row_peaks = jnp.maximum(lax.optimization_barrier(jnp.max(scores_pre, axis=1)), lax.optimization_barrier(jnp.max(scores_own, axis=1)))
        totals = lax.optimization_barrier(jnp.sum(jnp.exp(scores_pre - row_peaks[:, None]), axis=1)) + lax.optimization_barrier(jnp.sum(jnp.exp(scores_own - row_peaks[:, None]), axis=1))
        log_total = row_peaks + jnp.log(totals)
        weights_pre = jnp.exp(scores_pre - log_total[:, None])
        weights_own = jnp.exp(scores_own - log_total[:, None])
        slope_pre = jnp.dot(grad_rows, head_values.T, preferred_element_type=jnp.float32)
        slope_own = jnp.einsum('sqgd,skd->sqgk', grad_four.astype(jnp.float32), own_values.astype(jnp.float32)).reshape(-1, RL)
        centre = lax.optimization_barrier(jnp.sum(weights_pre * slope_pre, axis=1)) + lax.optimization_barrier(jnp.sum(weights_own * slope_own, axis=1))
        shift_pre = (weights_pre * (slope_pre - centre[:, None])).astype(jnp.bfloat16)
        shift_own = (weights_own * (slope_own - centre[:, None])).astype(jnp.bfloat16)
        shift_four = shift_own.reshape(SLOTS, RL, group_size, RL).astype(jnp.float32)
        weight_four = weights_own.astype(jnp.bfloat16).reshape(SLOTS, RL, group_size, RL).astype(jnp.float32)
        own_query = jnp.einsum('sqgk,skd->sqgd', shift_four, own_keys.astype(jnp.float32)) * scaling
        own_key = jnp.einsum('sqgk,sqgd->skd', shift_four, query_four.astype(jnp.float32)) * scaling
        own_value = jnp.einsum('sqgk,sqgd->skd', weight_four, grad_four.astype(jnp.float32))
        query_total = jnp.dot(shift_pre, head_keys, preferred_element_type=jnp.float32) * scaling + own_query.reshape(-1, HEAD_DIM)
        query_grads.append(query_total.reshape(SLOTS, RL, group_width))
        key_grads.append(own_key)
        value_grads.append(own_value)
        prefix_key_parts.append(block_sum(shift_pre, query_rows, scaling))
        prefix_value_parts.append(block_sum(weights_pre.astype(jnp.bfloat16), grad_rows, 1.0))
    grad_queries = jnp.concatenate(query_grads, axis=2).astype(jnp.bfloat16)
    grad_resp_keys = jnp.concatenate(key_grads, axis=2).astype(jnp.bfloat16)
    grad_resp_values = jnp.concatenate(value_grads, axis=2).astype(jnp.bfloat16)
    grad_prefix_keys = jnp.concatenate(prefix_key_parts, axis=1).astype(jnp.bfloat16)
    grad_prefix_values = jnp.concatenate(prefix_value_parts, axis=1).astype(jnp.bfloat16)
    return (grad_queries, grad_resp_keys, grad_resp_values, grad_prefix_keys, grad_prefix_values, forget_loss)

def reference(queries, cotangent, resp_keys, resp_values, prefix_keys, prefix_values, counts, lengths, policy_likelihood, reference_likelihood):
    results = lax.map(prompt_terms, (queries, cotangent, resp_keys, resp_values, prefix_keys, prefix_values, counts, lengths, policy_likelihood, reference_likelihood))
    return (results[0], results[1], results[2], results[3], results[4], results[5])
```

```python
import functools
import math

import jax
import jax.numpy as jnp
from jax import lax
from jax.experimental import pallas as pl
from jax.experimental.pallas import tpu as pltpu
from jax.sharding import PartitionSpec as P

HEADS = 64
KV_HEADS = 4
HEAD_DIM = 128


loss_beta = 0.5
masked_score = -1e30


def attention_kernel(n_pieces, factor_ref, q_ref, cot_ref, kown_ref, vown_ref, *rest):
    piece_refs = rest[:n_pieces]
    dq_ref, dkown_ref, dvown_ref = rest[n_pieces:n_pieces + 3]
    part_refs = rest[n_pieces + 3:]
    group_size = HEADS // KV_HEADS
    group_width = group_size * HEAD_DIM
    kv_width = KV_HEADS * HEAD_DIM
    resp_len = q_ref.shape[0]
    piece_len = piece_refs[0].shape[0]
    scaling = 1.0 / math.sqrt(HEAD_DIM)
    rows = group_size * resp_len
    factor = factor_ref[...]
    token_of_row = lax.broadcasted_iota(jnp.int32, (rows, resp_len), 0) % resp_len
    own_pos = lax.broadcasted_iota(jnp.int32, (rows, resp_len), 1)
    causal = token_of_row >= own_pos
    contract_rows = (((0,), (0,)), ((), ()))
    contract_cols = (((1,), (1,)), ((), ()))
    for g in range(KV_HEADS):
        base = g * group_width
        q_rows = jnp.concatenate(
            [q_ref[:, base + h * HEAD_DIM:base + (h + 1) * HEAD_DIM] for h in range(group_size)], axis=0
        )
        g_rows = jnp.concatenate(
            [
                (cot_ref[:, base + h * HEAD_DIM:base + (h + 1) * HEAD_DIM].astype(jnp.float32) * factor).astype(
                    jnp.bfloat16
                )
                for h in range(group_size)
            ],
            axis=0,
        )
        k_cols = slice(g * HEAD_DIM, (g + 1) * HEAD_DIM)
        v_cols = slice(kv_width + g * HEAD_DIM, kv_width + (g + 1) * HEAD_DIM)
        k_pre = jnp.concatenate([r[:, k_cols] for r in piece_refs], axis=0)
        v_pre = jnp.concatenate([r[:, v_cols] for r in piece_refs], axis=0)
        k_own = kown_ref[:, k_cols]
        v_own = vown_ref[:, k_cols]
        s_pre = lax.dot_general(q_rows, k_pre, contract_cols, preferred_element_type=jnp.float32) * scaling
        s_own = lax.dot_general(q_rows, k_own, contract_cols, preferred_element_type=jnp.float32) * scaling
        s_own = jnp.where(causal, s_own, masked_score)
        peak = jnp.maximum(jnp.max(s_pre, axis=1, keepdims=True), jnp.max(s_own, axis=1, keepdims=True))
        total = jnp.sum(jnp.exp(s_pre - peak), axis=1, keepdims=True) + jnp.sum(
            jnp.exp(s_own - peak), axis=1, keepdims=True
        )
        log_total = peak + jnp.log(total)
        p_pre = jnp.exp(s_pre - log_total)
        p_own = jnp.exp(s_own - log_total)
        dp_pre = lax.dot_general(g_rows, v_pre, contract_cols, preferred_element_type=jnp.float32)
        dp_own = lax.dot_general(g_rows, v_own, contract_cols, preferred_element_type=jnp.float32)
        centre = jnp.sum(p_pre * dp_pre, axis=1, keepdims=True) + jnp.sum(p_own * dp_own, axis=1, keepdims=True)
        ds_pre = (p_pre * (dp_pre - centre)).astype(jnp.bfloat16)
        ds_own = (p_own * (dp_own - centre)).astype(jnp.bfloat16)
        pl_pre = p_pre.astype(jnp.bfloat16)
        pl_own = p_own.astype(jnp.bfloat16)
        dq_rows = (
            jnp.dot(ds_pre, k_pre, preferred_element_type=jnp.float32) * scaling
            + jnp.dot(ds_own, k_own, preferred_element_type=jnp.float32) * scaling
        )
        for h in range(group_size):
            dq_ref[:, base + h * HEAD_DIM:base + (h + 1) * HEAD_DIM] = dq_rows[
                h * resp_len:(h + 1) * resp_len
            ].astype(jnp.bfloat16)
        dk_own = lax.dot_general(ds_own, q_rows, contract_rows, preferred_element_type=jnp.float32) * scaling
        dv_own = lax.dot_general(pl_own, g_rows, contract_rows, preferred_element_type=jnp.float32)
        dkown_ref[:, k_cols] = dk_own.astype(jnp.bfloat16)
        dvown_ref[:, k_cols] = dv_own.astype(jnp.bfloat16)
        dk_pre = lax.dot_general(ds_pre, q_rows, contract_rows, preferred_element_type=jnp.float32) * scaling
        dv_pre = lax.dot_general(pl_pre, g_rows, contract_rows, preferred_element_type=jnp.float32)
        for i, r in enumerate(part_refs):
            r[:, k_cols] = dk_pre[i * piece_len:(i + 1) * piece_len].astype(jnp.bfloat16)
            r[:, v_cols] = dv_pre[i * piece_len:(i + 1) * piece_len].astype(jnp.bfloat16)


def shifted(value, shift, n):
    return lax.ppermute(value, "resp", [(i, (i + shift) % n) for i in range(n)])


def on_device(
    queries,
    cotangent,
    resp_keys,
    resp_values,
    prefix_keys,
    prefix_values,
    counts,
    lengths,
    policy_likelihood,
    reference_likelihood,
):
    n = lax.axis_size("resp")
    slot_count = queries.shape[1]
    assert slot_count == 1
    resp_len = queries.shape[2]
    piece_len = prefix_keys.shape[1]
    kv_width = KV_HEADS * HEAD_DIM
    local_kv = jnp.concatenate([prefix_keys[0], prefix_values[0]], axis=1)
    pieces = [local_kv] + [shifted(local_kv, k, n) for k in range(1, n)]
    live_count = counts[0]
    count_real = live_count.astype(jnp.float32)
    slot_ids = lax.axis_index("resp") * slot_count + jnp.arange(slot_count, dtype=jnp.int32)
    live_slots = slot_ids < live_count
    margin = policy_likelihood[0] - reference_likelihood[0]
    weight = jnp.where(live_slots, 2.0 * jax.nn.sigmoid(loss_beta * margin) / count_real, 0.0)
    loss_terms = jnp.where(live_slots, 2.0 / loss_beta * jax.nn.softplus(loss_beta * margin), 0.0)
    all_terms = [loss_terms] + [shifted(loss_terms, k, n) for k in range(1, n)]
    forget_loss = (jnp.sum(jnp.concatenate(all_terms)) / count_real).reshape(1)
    positions = jnp.arange(resp_len, dtype=jnp.int32)
    factor = jnp.where(positions[None, :] < lengths[0][:, None], weight[:, None], 0.0)
    factor = factor.reshape(resp_len, 1).astype(jnp.float32)
    out_shape = (
        jax.ShapeDtypeStruct(queries.shape[2:], jnp.bfloat16),
        jax.ShapeDtypeStruct(resp_keys.shape[2:], jnp.bfloat16),
        jax.ShapeDtypeStruct(resp_values.shape[2:], jnp.bfloat16),
    ) + tuple(jax.ShapeDtypeStruct((piece_len, 2 * kv_width), jnp.bfloat16) for _ in range(n))
    results = pl.pallas_call(
        functools.partial(attention_kernel, n),
        out_shape=out_shape,
    )(factor, queries[0, 0], cotangent[0, 0], resp_keys[0, 0], resp_values[0, 0], *pieces)
    grad_q, grad_k, grad_v = results[:3]
    parts = results[3:]
    summed = parts[0].astype(jnp.float32)
    for k in range(1, n):
        summed = summed + shifted(parts[k], -k, n).astype(jnp.float32)
    summed = summed.astype(jnp.bfloat16)
    return (
        grad_q[None, None],
        grad_k[None, None],
        grad_v[None, None],
        summed[:, :kv_width][None],
        summed[:, kv_width:][None],
        forget_loss,
    )


def solution(mesh):
    placed = (
        P(("groups", "prompt"), "resp", None, None),
        P(("groups", "prompt"), "resp", None, None),
        P(("groups", "prompt"), "resp", None, None),
        P(("groups", "prompt"), "resp", None, None),
        P(("groups", "prompt"), "resp", None),
        P(("groups", "prompt"), "resp", None),
        P(("groups", "prompt")),
        P(("groups", "prompt"), "resp"),
        P(("groups", "prompt"), "resp"),
        P(("groups", "prompt"), "resp"),
    )
    return jax.shard_map(
        on_device,
        mesh=mesh,
        in_specs=placed,
        out_specs=(
            P(("groups", "prompt"), "resp", None, None),
            P(("groups", "prompt"), "resp", None, None),
            P(("groups", "prompt"), "resp", None, None),
            P(("groups", "prompt"), "resp", None),
            P(("groups", "prompt"), "resp", None),
            P(("groups", "prompt")),
        ),
        check_vma=False,
    )
```

```python
import functools
import math

import jax
import jax.numpy as jnp
from jax import lax
from jax.experimental import pallas as pl
from jax.experimental.pallas import tpu as pltpu
from jax.sharding import PartitionSpec as P

HEADS = 64
KV_HEADS = 4
HEAD_DIM = 128


loss_beta = 0.5
masked_score = -1e30


def slot_columns(refs, columns):
    if len(refs) == 1:
        return refs[0][:, columns]
    total = refs[0][:, columns].astype(jnp.float32)
    for r in refs[1:]:
        total = total + r[:, columns].astype(jnp.float32)
    return total.astype(jnp.bfloat16)


def attention_kernel(slot_spec, factor_ref, q_ref, cot_ref, kown_ref, vown_ref, *rest):
    n_inputs = sum(len(s) for s in slot_spec)
    input_refs = rest[:n_inputs]
    piece_refs = [[input_refs[i] for i in s] for s in slot_spec]
    dq_ref, dkown_ref, dvown_ref = rest[n_inputs:n_inputs + 3]
    part_refs = rest[n_inputs + 3:]
    group_size = HEADS // KV_HEADS
    group_width = group_size * HEAD_DIM
    kv_width = KV_HEADS * HEAD_DIM
    resp_len = q_ref.shape[0]
    piece_len = input_refs[0].shape[0]
    scaling = 1.0 / math.sqrt(HEAD_DIM)
    rows = group_size * resp_len
    factor = factor_ref[...]
    token_of_row = lax.broadcasted_iota(jnp.int32, (rows, resp_len), 0) % resp_len
    own_pos = lax.broadcasted_iota(jnp.int32, (rows, resp_len), 1)
    causal = token_of_row >= own_pos
    contract_rows = (((0,), (0,)), ((), ()))
    contract_cols = (((1,), (1,)), ((), ()))
    for g in range(KV_HEADS):
        base = g * group_width
        q_rows = jnp.concatenate(
            [q_ref[:, base + h * HEAD_DIM:base + (h + 1) * HEAD_DIM] for h in range(group_size)], axis=0
        )
        g_rows = jnp.concatenate(
            [
                (cot_ref[:, base + h * HEAD_DIM:base + (h + 1) * HEAD_DIM].astype(jnp.float32) * factor).astype(
                    jnp.bfloat16
                )
                for h in range(group_size)
            ],
            axis=0,
        )
        k_cols = slice(g * HEAD_DIM, (g + 1) * HEAD_DIM)
        v_cols = slice(kv_width + g * HEAD_DIM, kv_width + (g + 1) * HEAD_DIM)
        k_pre = jnp.concatenate([slot_columns(r, k_cols) for r in piece_refs], axis=0)
        v_pre = jnp.concatenate([slot_columns(r, v_cols) for r in piece_refs], axis=0)
        k_own = kown_ref[:, k_cols]
        v_own = vown_ref[:, k_cols]
        s_pre = lax.dot_general(q_rows, k_pre, contract_cols, preferred_element_type=jnp.float32) * scaling
        s_own = lax.dot_general(q_rows, k_own, contract_cols, preferred_element_type=jnp.float32) * scaling
        s_own = jnp.where(causal, s_own, masked_score)
        peak = jnp.maximum(jnp.max(s_pre, axis=1, keepdims=True), jnp.max(s_own, axis=1, keepdims=True))
        total = jnp.sum(jnp.exp(s_pre - peak), axis=1, keepdims=True) + jnp.sum(
            jnp.exp(s_own - peak), axis=1, keepdims=True
        )
        log_total = peak + jnp.log(total)
        p_pre = jnp.exp(s_pre - log_total)
        p_own = jnp.exp(s_own - log_total)
        dp_pre = lax.dot_general(g_rows, v_pre, contract_cols, preferred_element_type=jnp.float32)
        dp_own = lax.dot_general(g_rows, v_own, contract_cols, preferred_element_type=jnp.float32)
        centre = jnp.sum(p_pre * dp_pre, axis=1, keepdims=True) + jnp.sum(p_own * dp_own, axis=1, keepdims=True)
        ds_pre = (p_pre * (dp_pre - centre)).astype(jnp.bfloat16)
        ds_own = (p_own * (dp_own - centre)).astype(jnp.bfloat16)
        pl_pre = p_pre.astype(jnp.bfloat16)
        pl_own = p_own.astype(jnp.bfloat16)
        dq_rows = (
            jnp.dot(ds_pre, k_pre, preferred_element_type=jnp.float32) * scaling
            + jnp.dot(ds_own, k_own, preferred_element_type=jnp.float32) * scaling
        )
        for h in range(group_size):
            dq_ref[:, base + h * HEAD_DIM:base + (h + 1) * HEAD_DIM] = dq_rows[
                h * resp_len:(h + 1) * resp_len
            ].astype(jnp.bfloat16)
        dk_own = lax.dot_general(ds_own, q_rows, contract_rows, preferred_element_type=jnp.float32) * scaling
        dv_own = lax.dot_general(pl_own, g_rows, contract_rows, preferred_element_type=jnp.float32)
        dkown_ref[:, k_cols] = dk_own.astype(jnp.bfloat16)
        dvown_ref[:, k_cols] = dv_own.astype(jnp.bfloat16)
        dk_pre = lax.dot_general(ds_pre, q_rows, contract_rows, preferred_element_type=jnp.float32) * scaling
        dv_pre = lax.dot_general(pl_pre, g_rows, contract_rows, preferred_element_type=jnp.float32)
        for i, r in enumerate(part_refs):
            r[:, k_cols] = dk_pre[i * piece_len:(i + 1) * piece_len].astype(jnp.bfloat16)
            r[:, v_cols] = dv_pre[i * piece_len:(i + 1) * piece_len].astype(jnp.bfloat16)


def shifted(value, shift, n):
    return lax.ppermute(value, "resp", [(i, (i + shift) % n) for i in range(n)])


def moved(value, pairs):
    return lax.ppermute(value, "resp", pairs)


def line_pairs(n, shift):
    return [(i, i + shift) for i in range(n) if 0 <= i + shift < n]


def gather_line4(local):
    right_one = moved(local, line_pairs(4, 1))
    left_one = moved(local, line_pairs(4, -1))
    right_two = moved(local, line_pairs(4, 2))
    left_two = moved(local, line_pairs(4, -2))
    fwd_right = moved(right_two, [(2, 3)])
    fwd_left = moved(left_two, [(1, 0)])
    return [local, (right_one, fwd_left), (left_one, fwd_right), (right_two, left_two)]


def scatter_line4(parts):
    own, slot_one, slot_two, slot_three = parts
    fwd_right = moved(slot_one, [(0, 1)])
    fwd_left = moved(slot_two, [(3, 2)])
    left_one = moved(slot_one, line_pairs(4, -1))
    right_one = moved(slot_two, line_pairs(4, 1))
    merged = (
        slot_three.astype(jnp.float32) + fwd_right.astype(jnp.float32) + fwd_left.astype(jnp.float32)
    ).astype(jnp.bfloat16)
    right_two = moved(merged, line_pairs(4, 2))
    left_two = moved(merged, line_pairs(4, -2))
    total = own.astype(jnp.float32)
    for piece in (left_one, right_one, right_two, left_two):
        total = total + piece.astype(jnp.float32)
    return total


def on_device(
    queries,
    cotangent,
    resp_keys,
    resp_values,
    prefix_keys,
    prefix_values,
    counts,
    lengths,
    policy_likelihood,
    reference_likelihood,
):
    n = lax.axis_size("resp")
    slot_count = queries.shape[1]
    assert slot_count == 1
    resp_len = queries.shape[2]
    piece_len = prefix_keys.shape[1]
    kv_width = KV_HEADS * HEAD_DIM
    local_kv = jnp.concatenate([prefix_keys[0], prefix_values[0]], axis=1)
    if n == 4:
        slots = gather_line4(local_kv)
    else:
        slots = [local_kv] + [shifted(local_kv, k, n) for k in range(1, n)]
    slots = [s if isinstance(s, tuple) else (s,) for s in slots]
    slot_spec = []
    pieces = []
    for s in slots:
        slot_spec.append(tuple(range(len(pieces), len(pieces) + len(s))))
        pieces.extend(s)
    live_count = counts[0]
    count_real = live_count.astype(jnp.float32)
    slot_ids = lax.axis_index("resp") * slot_count + jnp.arange(slot_count, dtype=jnp.int32)
    live_slots = slot_ids < live_count
    margin = policy_likelihood[0] - reference_likelihood[0]
    weight = jnp.where(live_slots, 2.0 * jax.nn.sigmoid(loss_beta * margin) / count_real, 0.0)
    loss_terms = jnp.where(live_slots, 2.0 / loss_beta * jax.nn.softplus(loss_beta * margin), 0.0)
    all_terms = [loss_terms] + [shifted(loss_terms, k, n) for k in range(1, n)]
    forget_loss = (jnp.sum(jnp.concatenate(all_terms)) / count_real).reshape(1)
    positions = jnp.arange(resp_len, dtype=jnp.int32)
    factor = jnp.where(positions[None, :] < lengths[0][:, None], weight[:, None], 0.0)
    factor = factor.reshape(resp_len, 1).astype(jnp.float32)
    forget_loss, factor, *pieces = lax.optimization_barrier((forget_loss, factor, *pieces))
    out_shape = (
        jax.ShapeDtypeStruct(queries.shape[2:], jnp.bfloat16),
        jax.ShapeDtypeStruct(resp_keys.shape[2:], jnp.bfloat16),
        jax.ShapeDtypeStruct(resp_values.shape[2:], jnp.bfloat16),
    ) + tuple(jax.ShapeDtypeStruct((piece_len, 2 * kv_width), jnp.bfloat16) for _ in range(n))
    results = pl.pallas_call(
        functools.partial(attention_kernel, tuple(slot_spec)),
        out_shape=out_shape,
    )(factor, queries[0, 0], cotangent[0, 0], resp_keys[0, 0], resp_values[0, 0], *pieces)
    grad_q, grad_k, grad_v = results[:3]
    parts = results[3:]
    if n == 4:
        summed = scatter_line4(parts)
    else:
        summed = parts[0].astype(jnp.float32)
        for k in range(1, n):
            summed = summed + shifted(parts[k], -k, n).astype(jnp.float32)
    summed = summed.astype(jnp.bfloat16)
    return (
        grad_q[None, None],
        grad_k[None, None],
        grad_v[None, None],
        summed[:, :kv_width][None],
        summed[:, kv_width:][None],
        forget_loss,
    )


def solution(mesh):
    placed = (
        P(("groups", "prompt"), "resp", None, None),
        P(("groups", "prompt"), "resp", None, None),
        P(("groups", "prompt"), "resp", None, None),
        P(("groups", "prompt"), "resp", None, None),
        P(("groups", "prompt"), "resp", None),
        P(("groups", "prompt"), "resp", None),
        P(("groups", "prompt")),
        P(("groups", "prompt"), "resp"),
        P(("groups", "prompt"), "resp"),
        P(("groups", "prompt"), "resp"),
    )
    return jax.shard_map(
        on_device,
        mesh=mesh,
        in_specs=placed,
        out_specs=(
            P(("groups", "prompt"), "resp", None, None),
            P(("groups", "prompt"), "resp", None, None),
            P(("groups", "prompt"), "resp", None, None),
            P(("groups", "prompt"), "resp", None),
            P(("groups", "prompt"), "resp", None),
            P(("groups", "prompt")),
        ),
        check_vma=False,
    )
```

```python
import functools
import math

import jax
import jax.numpy as jnp
from jax import lax
from jax.experimental import pallas as pl
from jax.experimental.pallas import tpu as pltpu
from jax.sharding import PartitionSpec as P

HEADS = 64
KV_HEADS = 4
HEAD_DIM = 128


loss_beta = 0.5
masked_score = -1e30


def slot_columns(refs, columns):
    if len(refs) == 1:
        return refs[0][:, columns]
    total = refs[0][:, columns].astype(jnp.float32)
    for r in refs[1:]:
        total = total + r[:, columns].astype(jnp.float32)
    return total.astype(jnp.bfloat16)


def attention_kernel(slot_spec, factor_ref, q_ref, cot_ref, kown_ref, vown_ref, *rest):
    n_inputs = sum(len(s) for s in slot_spec)
    input_refs = rest[:n_inputs]
    piece_refs = [[input_refs[i] for i in s] for s in slot_spec]
    dq_ref, dkown_ref, dvown_ref = rest[n_inputs:n_inputs + 3]
    part_refs = rest[n_inputs + 3:]
    group_size = HEADS // KV_HEADS
    group_width = group_size * HEAD_DIM
    kv_width = KV_HEADS * HEAD_DIM
    resp_len = q_ref.shape[0]
    piece_len = input_refs[0].shape[0]
    scaling = 1.0 / math.sqrt(HEAD_DIM)
    rows = group_size * resp_len
    factor = factor_ref[...]
    token_of_row = lax.broadcasted_iota(jnp.int32, (rows, resp_len), 0) % resp_len
    own_pos = lax.broadcasted_iota(jnp.int32, (rows, resp_len), 1)
    causal = token_of_row >= own_pos
    contract_rows = (((0,), (0,)), ((), ()))
    contract_cols = (((1,), (1,)), ((), ()))
    for g in range(KV_HEADS):
        base = g * group_width
        q_rows = jnp.concatenate(
            [q_ref[:, base + h * HEAD_DIM:base + (h + 1) * HEAD_DIM] for h in range(group_size)], axis=0
        )
        g_rows = jnp.concatenate(
            [
                (cot_ref[:, base + h * HEAD_DIM:base + (h + 1) * HEAD_DIM].astype(jnp.float32) * factor).astype(
                    jnp.bfloat16
                )
                for h in range(group_size)
            ],
            axis=0,
        )
        k_cols = slice(g * HEAD_DIM, (g + 1) * HEAD_DIM)
        v_cols = slice(kv_width + g * HEAD_DIM, kv_width + (g + 1) * HEAD_DIM)
        k_pre = jnp.concatenate([slot_columns(r, k_cols) for r in piece_refs], axis=0)
        v_pre = jnp.concatenate([slot_columns(r, v_cols) for r in piece_refs], axis=0)
        k_own = kown_ref[:, k_cols]
        v_own = vown_ref[:, k_cols]
        s_pre = lax.dot_general(q_rows, k_pre, contract_cols, preferred_element_type=jnp.float32) * scaling
        s_own = lax.dot_general(q_rows, k_own, contract_cols, preferred_element_type=jnp.float32) * scaling
        s_own = jnp.where(causal, s_own, masked_score)
        peak = jnp.maximum(jnp.max(s_pre, axis=1, keepdims=True), jnp.max(s_own, axis=1, keepdims=True))
        total = jnp.sum(jnp.exp(s_pre - peak), axis=1, keepdims=True) + jnp.sum(
            jnp.exp(s_own - peak), axis=1, keepdims=True
        )
        log_total = peak + jnp.log(total)
        p_pre = jnp.exp(s_pre - log_total)
        p_own = jnp.exp(s_own - log_total)
        dp_pre = lax.dot_general(g_rows, v_pre, contract_cols, preferred_element_type=jnp.float32)
        dp_own = lax.dot_general(g_rows, v_own, contract_cols, preferred_element_type=jnp.float32)
        centre = jnp.sum(p_pre * dp_pre, axis=1, keepdims=True) + jnp.sum(p_own * dp_own, axis=1, keepdims=True)
        ds_pre = (p_pre * (dp_pre - centre)).astype(jnp.bfloat16)
        ds_own = (p_own * (dp_own - centre)).astype(jnp.bfloat16)
        pl_pre = p_pre.astype(jnp.bfloat16)
        pl_own = p_own.astype(jnp.bfloat16)
        dq_rows = (
            jnp.dot(ds_pre, k_pre, preferred_element_type=jnp.float32) * scaling
            + jnp.dot(ds_own, k_own, preferred_element_type=jnp.float32) * scaling
        )
        for h in range(group_size):
            dq_ref[:, base + h * HEAD_DIM:base + (h + 1) * HEAD_DIM] = dq_rows[
                h * resp_len:(h + 1) * resp_len
            ].astype(jnp.bfloat16)
        dk_own = lax.dot_general(ds_own, q_rows, contract_rows, preferred_element_type=jnp.float32) * scaling
        dv_own = lax.dot_general(pl_own, g_rows, contract_rows, preferred_element_type=jnp.float32)
        dkown_ref[:, k_cols] = dk_own.astype(jnp.bfloat16)
        dvown_ref[:, k_cols] = dv_own.astype(jnp.bfloat16)
        dk_pre = lax.dot_general(ds_pre, q_rows, contract_rows, preferred_element_type=jnp.float32) * scaling
        dv_pre = lax.dot_general(pl_pre, g_rows, contract_rows, preferred_element_type=jnp.float32)
        for i, r in enumerate(part_refs):
            r[:, k_cols] = dk_pre[i * piece_len:(i + 1) * piece_len].astype(jnp.bfloat16)
            r[:, v_cols] = dv_pre[i * piece_len:(i + 1) * piece_len].astype(jnp.bfloat16)


def shifted(value, shift, n):
    return lax.ppermute(value, "resp", [(i, (i + shift) % n) for i in range(n)])


def on_device(
    queries,
    cotangent,
    resp_keys,
    resp_values,
    prefix_keys,
    prefix_values,
    counts,
    lengths,
    policy_likelihood,
    reference_likelihood,
):
    n = lax.axis_size("resp")
    slot_count = queries.shape[1]
    assert slot_count == 1
    resp_len = queries.shape[2]
    piece_len = prefix_keys.shape[1]
    kv_width = KV_HEADS * HEAD_DIM
    local_kv = jnp.concatenate([prefix_keys[0], prefix_values[0]], axis=1)
    slots = [local_kv] + [shifted(local_kv, k, n) for k in range(1, n)]
    slots = [s if isinstance(s, tuple) else (s,) for s in slots]
    slot_spec = []
    pieces = []
    for s in slots:
        slot_spec.append(tuple(range(len(pieces), len(pieces) + len(s))))
        pieces.extend(s)
    live_count = counts[0]
    count_real = live_count.astype(jnp.float32)
    slot_ids = lax.axis_index("resp") * slot_count + jnp.arange(slot_count, dtype=jnp.int32)
    live_slots = slot_ids < live_count
    margin = policy_likelihood[0] - reference_likelihood[0]
    weight = jnp.where(live_slots, 2.0 * jax.nn.sigmoid(loss_beta * margin) / count_real, 0.0)
    loss_terms = jnp.where(live_slots, 2.0 / loss_beta * jax.nn.softplus(loss_beta * margin), 0.0)
    forget_loss = (lax.psum(jnp.sum(loss_terms), "resp") / count_real).reshape(1)
    positions = jnp.arange(resp_len, dtype=jnp.int32)
    factor = jnp.where(positions[None, :] < lengths[0][:, None], weight[:, None], 0.0)
    factor = factor.reshape(resp_len, 1).astype(jnp.float32)
    forget_loss, factor, *pieces = lax.optimization_barrier((forget_loss, factor, *pieces))
    out_shape = (
        jax.ShapeDtypeStruct(queries.shape[2:], jnp.bfloat16),
        jax.ShapeDtypeStruct(resp_keys.shape[2:], jnp.bfloat16),
        jax.ShapeDtypeStruct(resp_values.shape[2:], jnp.bfloat16),
    ) + tuple(jax.ShapeDtypeStruct((piece_len, 2 * kv_width), jnp.bfloat16) for _ in range(n))
    results = pl.pallas_call(
        functools.partial(attention_kernel, tuple(slot_spec)),
        out_shape=out_shape,
    )(factor, queries[0, 0], cotangent[0, 0], resp_keys[0, 0], resp_values[0, 0], *pieces)
    grad_q, grad_k, grad_v = results[:3]
    parts = results[3:]
    summed = parts[0].astype(jnp.float32)
    for k in range(1, n):
        summed = summed + shifted(parts[k], -k, n).astype(jnp.float32)
    summed = summed.astype(jnp.bfloat16)
    return (
        grad_q[None, None],
        grad_k[None, None],
        grad_v[None, None],
        summed[:, :kv_width][None],
        summed[:, kv_width:][None],
        forget_loss,
    )


def solution(mesh):
    placed = (
        P(("groups", "prompt"), "resp", None, None),
        P(("groups", "prompt"), "resp", None, None),
        P(("groups", "prompt"), "resp", None, None),
        P(("groups", "prompt"), "resp", None, None),
        P(("groups", "prompt"), "resp", None),
        P(("groups", "prompt"), "resp", None),
        P(("groups", "prompt")),
        P(("groups", "prompt"), "resp"),
        P(("groups", "prompt"), "resp"),
        P(("groups", "prompt"), "resp"),
    )
    return jax.shard_map(
        on_device,
        mesh=mesh,
        in_specs=placed,
        out_specs=(
            P(("groups", "prompt"), "resp", None, None),
            P(("groups", "prompt"), "resp", None, None),
            P(("groups", "prompt"), "resp", None, None),
            P(("groups", "prompt"), "resp", None),
            P(("groups", "prompt"), "resp", None),
            P(("groups", "prompt")),
        ),
        check_vma=False,
    )
```

```python
import functools
import math

import jax
import jax.numpy as jnp
from jax import lax
from jax.experimental import pallas as pl
from jax.experimental.pallas import tpu as pltpu
from jax.sharding import PartitionSpec as P

HEADS = 64
KV_HEADS = 4
HEAD_DIM = 128


loss_beta = 0.5
masked_score = -1e30


def attention_kernel(n_pieces, factor_ref, q_ref, cot_ref, kown_ref, vown_ref, *rest):
    piece_refs = rest[:n_pieces]
    dq_ref, dkown_ref, dvown_ref = rest[n_pieces:n_pieces + 3]
    part_refs = rest[n_pieces + 3:]
    group_size = HEADS // KV_HEADS
    resp_len = q_ref.shape[0]
    piece_len = piece_refs[0].shape[1]
    scaling = 1.0 / math.sqrt(HEAD_DIM)
    rows = group_size * resp_len
    factor = factor_ref[...]
    contract_minor = (((1,), (1,)), ((), ()))
    contract_major = (((0,), (0,)), ((), ()))
    q_all = q_ref[...]
    g_all = (cot_ref[...].astype(jnp.float32) * factor).astype(jnp.bfloat16)
    q_rows = jnp.concatenate([q_all[:, h * HEAD_DIM:(h + 1) * HEAD_DIM] for h in range(group_size)], axis=0)
    g_rows = jnp.concatenate([g_all[:, h * HEAD_DIM:(h + 1) * HEAD_DIM] for h in range(group_size)], axis=0)
    k_pre = jnp.concatenate([r[0] for r in piece_refs], axis=0)
    v_pre = jnp.concatenate([r[1] for r in piece_refs], axis=0)
    k_own = kown_ref[...]
    v_own = vown_ref[...]
    s_pre = lax.dot_general(k_pre, q_rows, contract_minor, preferred_element_type=jnp.float32) * scaling
    s_own = lax.dot_general(k_own, q_rows, contract_minor, preferred_element_type=jnp.float32) * scaling
    own_pos = lax.broadcasted_iota(jnp.int32, (resp_len, rows), 0)
    token_of_col = lax.broadcasted_iota(jnp.int32, (resp_len, rows), 1) % resp_len
    s_own = jnp.where(token_of_col >= own_pos, s_own, masked_score)
    peak = jnp.maximum(jnp.max(s_pre, axis=0, keepdims=True), jnp.max(s_own, axis=0, keepdims=True))
    e_pre = jnp.exp(s_pre - peak)
    e_own = jnp.exp(s_own - peak)
    total = jnp.sum(e_pre, axis=0, keepdims=True) + jnp.sum(e_own, axis=0, keepdims=True)
    inv_total = 1.0 / total
    p_pre = e_pre * inv_total
    p_own = e_own * inv_total
    dp_pre = lax.dot_general(v_pre, g_rows, contract_minor, preferred_element_type=jnp.float32)
    dp_own = lax.dot_general(v_own, g_rows, contract_minor, preferred_element_type=jnp.float32)
    centre = jnp.sum(p_pre * dp_pre, axis=0, keepdims=True) + jnp.sum(p_own * dp_own, axis=0, keepdims=True)
    ds_pre = (p_pre * (dp_pre - centre)).astype(jnp.bfloat16)
    ds_own = (p_own * (dp_own - centre)).astype(jnp.bfloat16)
    dk_pre = jnp.dot(ds_pre, q_rows, preferred_element_type=jnp.float32) * scaling
    dv_pre = jnp.dot(p_pre.astype(jnp.bfloat16), g_rows, preferred_element_type=jnp.float32)
    for i, r in enumerate(part_refs):
        r[0] = dk_pre[i * piece_len:(i + 1) * piece_len].astype(jnp.bfloat16)
        r[1] = dv_pre[i * piece_len:(i + 1) * piece_len].astype(jnp.bfloat16)
    dkown_ref[...] = (jnp.dot(ds_own, q_rows, preferred_element_type=jnp.float32) * scaling).astype(jnp.bfloat16)
    dvown_ref[...] = jnp.dot(p_own.astype(jnp.bfloat16), g_rows, preferred_element_type=jnp.float32).astype(
        jnp.bfloat16
    )
    dq_rows = (
        lax.dot_general(ds_pre, k_pre, contract_major, preferred_element_type=jnp.float32) * scaling
        + lax.dot_general(ds_own, k_own, contract_major, preferred_element_type=jnp.float32) * scaling
    )
    for h in range(group_size):
        dq_ref[:, h * HEAD_DIM:(h + 1) * HEAD_DIM] = dq_rows[h * resp_len:(h + 1) * resp_len].astype(jnp.bfloat16)


def shifted(value, shift, n):
    return lax.ppermute(value, "resp", [(i, (i + shift) % n) for i in range(n)])


def on_device(
    queries,
    cotangent,
    resp_keys,
    resp_values,
    prefix_keys,
    prefix_values,
    counts,
    lengths,
    policy_likelihood,
    reference_likelihood,
):
    n = lax.axis_size("resp")
    slot_count = queries.shape[1]
    assert slot_count == 1
    resp_len = queries.shape[2]
    piece_len = prefix_keys.shape[1]
    local_kv = jnp.stack([prefix_keys[0], prefix_values[0]])
    pieces = [local_kv] + [shifted(local_kv, k, n) for k in range(1, n)]
    live_count = counts[0]
    count_real = live_count.astype(jnp.float32)
    slot_ids = lax.axis_index("resp") * slot_count + jnp.arange(slot_count, dtype=jnp.int32)
    live_slots = slot_ids < live_count
    margin = policy_likelihood[0] - reference_likelihood[0]
    weight = jnp.where(live_slots, 2.0 * jax.nn.sigmoid(loss_beta * margin) / count_real, 0.0)
    loss_terms = jnp.where(live_slots, 2.0 / loss_beta * jax.nn.softplus(loss_beta * margin), 0.0)
    forget_loss = (lax.psum(jnp.sum(loss_terms), "resp") / count_real).reshape(1)
    positions = jnp.arange(resp_len, dtype=jnp.int32)
    factor = jnp.where(positions[None, :] < lengths[0][:, None], weight[:, None], 0.0)
    factor = factor.reshape(resp_len, 1).astype(jnp.float32)
    forget_loss, factor, *pieces = lax.optimization_barrier((forget_loss, factor, *pieces))
    group_width = (HEADS // KV_HEADS) * HEAD_DIM
    piece_block = pl.BlockSpec((2, piece_len, HEAD_DIM), lambda g: (0, 0, g))
    results = pl.pallas_call(
        functools.partial(attention_kernel, n),
        grid=(KV_HEADS,),
        in_specs=[
            pl.BlockSpec((resp_len, 1), lambda g: (0, 0)),
            pl.BlockSpec((resp_len, group_width), lambda g: (0, g)),
            pl.BlockSpec((resp_len, group_width), lambda g: (0, g)),
            pl.BlockSpec((resp_len, HEAD_DIM), lambda g: (0, g)),
            pl.BlockSpec((resp_len, HEAD_DIM), lambda g: (0, g)),
        ]
        + [piece_block] * n,
        out_specs=[
            pl.BlockSpec((resp_len, group_width), lambda g: (0, g)),
            pl.BlockSpec((resp_len, HEAD_DIM), lambda g: (0, g)),
            pl.BlockSpec((resp_len, HEAD_DIM), lambda g: (0, g)),
        ]
        + [piece_block] * n,
        out_shape=[
            jax.ShapeDtypeStruct(queries.shape[2:], jnp.bfloat16),
            jax.ShapeDtypeStruct(resp_keys.shape[2:], jnp.bfloat16),
            jax.ShapeDtypeStruct(resp_values.shape[2:], jnp.bfloat16),
        ]
        + [jax.ShapeDtypeStruct(local_kv.shape, jnp.bfloat16) for _ in range(n)],
    )(factor, queries[0, 0], cotangent[0, 0], resp_keys[0, 0], resp_values[0, 0], *pieces)
    grad_q, grad_k, grad_v = results[:3]
    parts = results[3:]
    returned = [parts[0]] + [shifted(parts[k], -k, n) for k in range(1, n)]
    summed_keys = sum(r[0].astype(jnp.float32) for r in returned).astype(jnp.bfloat16)
    summed_values = sum(r[1].astype(jnp.float32) for r in returned).astype(jnp.bfloat16)
    return (
        grad_q[None, None],
        grad_k[None, None],
        grad_v[None, None],
        summed_keys[None],
        summed_values[None],
        forget_loss,
    )


def solution(mesh):
    placed = (
        P(("groups", "prompt"), "resp", None, None),
        P(("groups", "prompt"), "resp", None, None),
        P(("groups", "prompt"), "resp", None, None),
        P(("groups", "prompt"), "resp", None, None),
        P(("groups", "prompt"), "resp", None),
        P(("groups", "prompt"), "resp", None),
        P(("groups", "prompt")),
        P(("groups", "prompt"), "resp"),
        P(("groups", "prompt"), "resp"),
        P(("groups", "prompt"), "resp"),
    )
    return jax.shard_map(
        on_device,
        mesh=mesh,
        in_specs=placed,
        out_specs=(
            P(("groups", "prompt"), "resp", None, None),
            P(("groups", "prompt"), "resp", None, None),
            P(("groups", "prompt"), "resp", None, None),
            P(("groups", "prompt"), "resp", None),
            P(("groups", "prompt"), "resp", None),
            P(("groups", "prompt")),
        ),
        check_vma=False,
    )
```

```python
import functools
import math

import jax
import jax.numpy as jnp
from jax import lax
from jax.experimental import pallas as pl
from jax.experimental.pallas import tpu as pltpu
from jax.sharding import PartitionSpec as P

HEADS = 64
KV_HEADS = 4
HEAD_DIM = 128


loss_beta = 0.5
masked_score = -1e30


def attention_kernel(n_pieces, factor_ref, q_ref, cot_ref, kown_ref, vown_ref, *rest):
    piece_refs = rest[:n_pieces]
    dq_ref, dkown_ref, dvown_ref = rest[n_pieces:n_pieces + 3]
    part_refs = rest[n_pieces + 3:]
    group_size = HEADS // KV_HEADS
    resp_len = q_ref.shape[0]
    piece_len = piece_refs[0].shape[1]
    scaling = 1.0 / math.sqrt(HEAD_DIM)
    rows = group_size * resp_len
    factor = factor_ref[...]
    contract_minor = (((1,), (1,)), ((), ()))
    contract_major = (((0,), (0,)), ((), ()))
    q_all = q_ref[...]
    g_all = (cot_ref[...].astype(jnp.float32) * factor).astype(jnp.bfloat16)
    q_rows = jnp.concatenate([q_all[:, h * HEAD_DIM:(h + 1) * HEAD_DIM] for h in range(group_size)], axis=0)
    g_rows = jnp.concatenate([g_all[:, h * HEAD_DIM:(h + 1) * HEAD_DIM] for h in range(group_size)], axis=0)
    k_pre = jnp.concatenate([r[0] for r in piece_refs], axis=0)
    v_pre = jnp.concatenate([r[1] for r in piece_refs], axis=0)
    k_own = kown_ref[...]
    v_own = vown_ref[...]
    s_pre = lax.dot_general(k_pre, q_rows, contract_minor, preferred_element_type=jnp.float32) * scaling
    s_own = lax.dot_general(k_own, q_rows, contract_minor, preferred_element_type=jnp.float32) * scaling
    own_pos = lax.broadcasted_iota(jnp.int32, (resp_len, rows), 0)
    token_of_col = lax.broadcasted_iota(jnp.int32, (resp_len, rows), 1) % resp_len
    s_own = jnp.where(token_of_col >= own_pos, s_own, masked_score)
    peak = jnp.maximum(jnp.max(s_pre, axis=0, keepdims=True), jnp.max(s_own, axis=0, keepdims=True))
    e_pre = jnp.exp(s_pre - peak)
    e_own = jnp.exp(s_own - peak)
    total = jnp.sum(e_pre, axis=0, keepdims=True) + jnp.sum(e_own, axis=0, keepdims=True)
    inv_total = 1.0 / total
    p_pre = e_pre * inv_total
    p_own = e_own * inv_total
    dp_pre = lax.dot_general(v_pre, g_rows, contract_minor, preferred_element_type=jnp.float32)
    dp_own = lax.dot_general(v_own, g_rows, contract_minor, preferred_element_type=jnp.float32)
    centre = jnp.sum(p_pre * dp_pre, axis=0, keepdims=True) + jnp.sum(p_own * dp_own, axis=0, keepdims=True)
    ds_pre = (p_pre * (dp_pre - centre)).astype(jnp.bfloat16)
    ds_own = (p_own * (dp_own - centre)).astype(jnp.bfloat16)
    dk_pre = jnp.dot(ds_pre, q_rows, preferred_element_type=jnp.float32) * scaling
    dv_pre = jnp.dot(p_pre.astype(jnp.bfloat16), g_rows, preferred_element_type=jnp.float32)
    for i, r in enumerate(part_refs):
        r[0] = dk_pre[i * piece_len:(i + 1) * piece_len].astype(jnp.bfloat16)
        r[1] = dv_pre[i * piece_len:(i + 1) * piece_len].astype(jnp.bfloat16)
    dkown_ref[...] = (jnp.dot(ds_own, q_rows, preferred_element_type=jnp.float32) * scaling).astype(jnp.bfloat16)
    dvown_ref[...] = jnp.dot(p_own.astype(jnp.bfloat16), g_rows, preferred_element_type=jnp.float32).astype(
        jnp.bfloat16
    )
    dq_rows = (
        lax.dot_general(ds_pre, k_pre, contract_major, preferred_element_type=jnp.float32) * scaling
        + lax.dot_general(ds_own, k_own, contract_major, preferred_element_type=jnp.float32) * scaling
    )
    for h in range(group_size):
        dq_ref[:, h * HEAD_DIM:(h + 1) * HEAD_DIM] = dq_rows[h * resp_len:(h + 1) * resp_len].astype(jnp.bfloat16)


def shifted(value, shift, n):
    return lax.ppermute(value, "resp", [(i, (i + shift) % n) for i in range(n)])


def on_device(
    queries,
    cotangent,
    resp_keys,
    resp_values,
    prefix_keys,
    prefix_values,
    counts,
    lengths,
    policy_likelihood,
    reference_likelihood,
):
    n = lax.axis_size("resp")
    slot_count = queries.shape[1]
    assert slot_count == 1
    resp_len = queries.shape[2]
    piece_len = prefix_keys.shape[1]
    local_kv = jnp.stack([prefix_keys[0], prefix_values[0]])
    if n == 4:
        from_left = shifted(local_kv, 1, n)
        pieces = [local_kv, from_left, shifted(local_kv, -1, n), shifted(from_left, 1, n)]
    else:
        pieces = [local_kv] + [shifted(local_kv, k, n) for k in range(1, n)]
    live_count = counts[0]
    count_real = live_count.astype(jnp.float32)
    slot_ids = lax.axis_index("resp") * slot_count + jnp.arange(slot_count, dtype=jnp.int32)
    live_slots = slot_ids < live_count
    margin = policy_likelihood[0] - reference_likelihood[0]
    weight = jnp.where(live_slots, 2.0 * jax.nn.sigmoid(loss_beta * margin) / count_real, 0.0)
    loss_terms = jnp.where(live_slots, 2.0 / loss_beta * jax.nn.softplus(loss_beta * margin), 0.0)
    forget_loss = (lax.psum(jnp.sum(loss_terms), "resp") / count_real).reshape(1)
    positions = jnp.arange(resp_len, dtype=jnp.int32)
    factor = jnp.where(positions[None, :] < lengths[0][:, None], weight[:, None], 0.0)
    factor = factor.reshape(resp_len, 1).astype(jnp.float32)
    forget_loss, factor, *pieces = lax.optimization_barrier((forget_loss, factor, *pieces))
    group_width = (HEADS // KV_HEADS) * HEAD_DIM
    piece_block = pl.BlockSpec((2, piece_len, HEAD_DIM), lambda g: (0, 0, g))
    results = pl.pallas_call(
        functools.partial(attention_kernel, n),
        grid=(KV_HEADS,),
        in_specs=[
            pl.BlockSpec((resp_len, 1), lambda g: (0, 0)),
            pl.BlockSpec((resp_len, group_width), lambda g: (0, g)),
            pl.BlockSpec((resp_len, group_width), lambda g: (0, g)),
            pl.BlockSpec((resp_len, HEAD_DIM), lambda g: (0, g)),
            pl.BlockSpec((resp_len, HEAD_DIM), lambda g: (0, g)),
        ]
        + [piece_block] * n,
        out_specs=[
            pl.BlockSpec((resp_len, group_width), lambda g: (0, g)),
            pl.BlockSpec((resp_len, HEAD_DIM), lambda g: (0, g)),
            pl.BlockSpec((resp_len, HEAD_DIM), lambda g: (0, g)),
        ]
        + [piece_block] * n,
        out_shape=[
            jax.ShapeDtypeStruct(queries.shape[2:], jnp.bfloat16),
            jax.ShapeDtypeStruct(resp_keys.shape[2:], jnp.bfloat16),
            jax.ShapeDtypeStruct(resp_values.shape[2:], jnp.bfloat16),
        ]
        + [jax.ShapeDtypeStruct(local_kv.shape, jnp.bfloat16) for _ in range(n)],
    )(factor, queries[0, 0], cotangent[0, 0], resp_keys[0, 0], resp_values[0, 0], *pieces)
    grad_q, grad_k, grad_v = results[:3]
    parts = results[3:]
    if n == 4:
        relayed = shifted(parts[3], -1, n)
        merged = (parts[1].astype(jnp.float32) + relayed.astype(jnp.float32)).astype(jnp.bfloat16)
        returned = [parts[0], shifted(parts[2], 1, n), shifted(merged, -1, n)]
    else:
        returned = [parts[0]] + [shifted(parts[k], -k, n) for k in range(1, n)]
    summed_keys = sum(r[0].astype(jnp.float32) for r in returned).astype(jnp.bfloat16)
    summed_values = sum(r[1].astype(jnp.float32) for r in returned).astype(jnp.bfloat16)
    return (
        grad_q[None, None],
        grad_k[None, None],
        grad_v[None, None],
        summed_keys[None],
        summed_values[None],
        forget_loss,
    )


def solution(mesh):
    placed = (
        P(("groups", "prompt"), "resp", None, None),
        P(("groups", "prompt"), "resp", None, None),
        P(("groups", "prompt"), "resp", None, None),
        P(("groups", "prompt"), "resp", None, None),
        P(("groups", "prompt"), "resp", None),
        P(("groups", "prompt"), "resp", None),
        P(("groups", "prompt")),
        P(("groups", "prompt"), "resp"),
        P(("groups", "prompt"), "resp"),
        P(("groups", "prompt"), "resp"),
    )
    return jax.shard_map(
        on_device,
        mesh=mesh,
        in_specs=placed,
        out_specs=(
            P(("groups", "prompt"), "resp", None, None),
            P(("groups", "prompt"), "resp", None, None),
            P(("groups", "prompt"), "resp", None, None),
            P(("groups", "prompt"), "resp", None),
            P(("groups", "prompt"), "resp", None),
            P(("groups", "prompt")),
        ),
        check_vma=False,
    )
```

```python
import functools
import math

import jax
import jax.numpy as jnp
from jax import lax
from jax.experimental import pallas as pl
from jax.experimental.pallas import tpu as pltpu
from jax.sharding import PartitionSpec as P

HEADS = 64
KV_HEADS = 4
HEAD_DIM = 128


loss_beta = 0.5
masked_score = -1e30


def attention_kernel(n_pieces, scalar_ref, q_ref, cot_ref, kown_ref, vown_ref, *rest):
    piece_refs = rest[:n_pieces]
    dq_ref, dkown_ref, dvown_ref = rest[n_pieces:n_pieces + 3]
    part_refs = rest[n_pieces + 3:-1]
    loss_ref = rest[-1]
    group_size = HEADS // KV_HEADS
    resp_len = q_ref.shape[0]
    piece_len = part_refs[0].shape[1]
    scaling = 1.0 / math.sqrt(HEAD_DIM)
    rows = group_size * resp_len
    token = lax.broadcasted_iota(jnp.int32, (resp_len, 1), 0).astype(jnp.float32)
    factor = jnp.where(token < scalar_ref[1], scalar_ref[0], 0.0)

    @pl.when(pl.program_id(0) == 0)
    def _():
        term_total = scalar_ref[2]
        for r in piece_refs[1:]:
            term_total = term_total + jnp.sum(r[0, piece_len:piece_len + 8, :].astype(jnp.float32))
        loss_ref[0] = term_total / scalar_ref[3]
    contract_minor = (((1,), (1,)), ((), ()))
    contract_major = (((0,), (0,)), ((), ()))
    q_all = q_ref[...]
    g_all = (cot_ref[...].astype(jnp.float32) * factor).astype(jnp.bfloat16)
    q_rows = jnp.concatenate([q_all[:, h * HEAD_DIM:(h + 1) * HEAD_DIM] for h in range(group_size)], axis=0)
    g_rows = jnp.concatenate([g_all[:, h * HEAD_DIM:(h + 1) * HEAD_DIM] for h in range(group_size)], axis=0)
    k_pre = jnp.concatenate([r[0, :piece_len] for r in piece_refs], axis=0)
    v_pre = jnp.concatenate([r[1, :piece_len] for r in piece_refs], axis=0)
    k_own = kown_ref[...]
    v_own = vown_ref[...]
    s_pre = lax.dot_general(k_pre, q_rows, contract_minor, preferred_element_type=jnp.float32) * scaling
    s_own = lax.dot_general(k_own, q_rows, contract_minor, preferred_element_type=jnp.float32) * scaling
    own_pos = lax.broadcasted_iota(jnp.int32, (resp_len, rows), 0)
    token_of_col = lax.broadcasted_iota(jnp.int32, (resp_len, rows), 1) % resp_len
    s_own = jnp.where(token_of_col >= own_pos, s_own, masked_score)
    peak = jnp.maximum(jnp.max(s_pre, axis=0, keepdims=True), jnp.max(s_own, axis=0, keepdims=True))
    e_pre = jnp.exp(s_pre - peak)
    e_own = jnp.exp(s_own - peak)
    total = jnp.sum(e_pre, axis=0, keepdims=True) + jnp.sum(e_own, axis=0, keepdims=True)
    inv_total = 1.0 / total
    p_pre = e_pre * inv_total
    p_own = e_own * inv_total
    dp_pre = lax.dot_general(v_pre, g_rows, contract_minor, preferred_element_type=jnp.float32)
    dp_own = lax.dot_general(v_own, g_rows, contract_minor, preferred_element_type=jnp.float32)
    centre = jnp.sum(p_pre * dp_pre, axis=0, keepdims=True) + jnp.sum(p_own * dp_own, axis=0, keepdims=True)
    ds_pre = (p_pre * (dp_pre - centre)).astype(jnp.bfloat16)
    ds_own = (p_own * (dp_own - centre)).astype(jnp.bfloat16)
    dk_pre = jnp.dot(ds_pre, q_rows, preferred_element_type=jnp.float32) * scaling
    dv_pre = jnp.dot(p_pre.astype(jnp.bfloat16), g_rows, preferred_element_type=jnp.float32)
    for i, r in enumerate(part_refs):
        r[0] = dk_pre[i * piece_len:(i + 1) * piece_len].astype(jnp.bfloat16)
        r[1] = dv_pre[i * piece_len:(i + 1) * piece_len].astype(jnp.bfloat16)
    dkown_ref[...] = (jnp.dot(ds_own, q_rows, preferred_element_type=jnp.float32) * scaling).astype(jnp.bfloat16)
    dvown_ref[...] = jnp.dot(p_own.astype(jnp.bfloat16), g_rows, preferred_element_type=jnp.float32).astype(
        jnp.bfloat16
    )
    dq_rows = (
        lax.dot_general(ds_pre, k_pre, contract_major, preferred_element_type=jnp.float32) * scaling
        + lax.dot_general(ds_own, k_own, contract_major, preferred_element_type=jnp.float32) * scaling
    )
    for h in range(group_size):
        dq_ref[:, h * HEAD_DIM:(h + 1) * HEAD_DIM] = dq_rows[h * resp_len:(h + 1) * resp_len].astype(jnp.bfloat16)


def split_words(value):
    high = value.astype(jnp.bfloat16)
    rest = value - high.astype(jnp.float32)
    middle = rest.astype(jnp.bfloat16)
    low = (rest - middle.astype(jnp.float32)).astype(jnp.bfloat16)
    return jnp.stack([high, middle, low])


def shifted(value, shift, n):
    return lax.ppermute(value, "resp", [(i, (i + shift) % n) for i in range(n)])


def on_device(
    queries,
    cotangent,
    resp_keys,
    resp_values,
    prefix_keys,
    prefix_values,
    counts,
    lengths,
    policy_likelihood,
    reference_likelihood,
):
    n = lax.axis_size("resp")
    slot_count = queries.shape[1]
    assert slot_count == 1
    resp_len = queries.shape[2]
    piece_len = prefix_keys.shape[1]
    live_count = counts[0]
    count_real = live_count.astype(jnp.float32)
    slot_ids = lax.axis_index("resp") * slot_count + jnp.arange(slot_count, dtype=jnp.int32)
    live_slots = slot_ids < live_count
    margin = policy_likelihood[0] - reference_likelihood[0]
    weight = jnp.where(live_slots, 2.0 * jax.nn.sigmoid(loss_beta * margin) / count_real, 0.0)
    loss_terms = jnp.where(live_slots, 2.0 / loss_beta * jax.nn.softplus(loss_beta * margin), 0.0)
    own_term = jnp.sum(loss_terms)
    word_rows = jnp.zeros((2, 16, prefix_keys.shape[2]), jnp.bfloat16)
    word_rows = word_rows.at[0, 0, 0:3].set(split_words(own_term))
    local_kv = jnp.concatenate([jnp.stack([prefix_keys[0], prefix_values[0]]), word_rows], axis=1)
    if n == 4:
        from_left = shifted(local_kv, 1, n)
        pieces = [local_kv, from_left, shifted(local_kv, -1, n), shifted(from_left, 1, n)]
    else:
        pieces = [local_kv] + [shifted(local_kv, k, n) for k in range(1, n)]
    scalars = jnp.stack([weight[0], lengths[0][0].astype(jnp.float32), own_term, count_real])
    group_width = (HEADS // KV_HEADS) * HEAD_DIM
    piece_block = pl.BlockSpec((2, piece_len + 16, HEAD_DIM), lambda g: (0, 0, g))
    part_block = pl.BlockSpec((2, piece_len, HEAD_DIM), lambda g: (0, 0, g))
    results = pl.pallas_call(
        functools.partial(attention_kernel, n),
        grid=(KV_HEADS,),
        in_specs=[
            pl.BlockSpec(memory_space=pltpu.SMEM),
            pl.BlockSpec((resp_len, group_width), lambda g: (0, g)),
            pl.BlockSpec((resp_len, group_width), lambda g: (0, g)),
            pl.BlockSpec((resp_len, HEAD_DIM), lambda g: (0, g)),
            pl.BlockSpec((resp_len, HEAD_DIM), lambda g: (0, g)),
        ]
        + [piece_block] * n,
        out_specs=[
            pl.BlockSpec((resp_len, group_width), lambda g: (0, g)),
            pl.BlockSpec((resp_len, HEAD_DIM), lambda g: (0, g)),
            pl.BlockSpec((resp_len, HEAD_DIM), lambda g: (0, g)),
        ]
        + [part_block] * n
        + [pl.BlockSpec(memory_space=pltpu.SMEM)],
        out_shape=[
            jax.ShapeDtypeStruct(queries.shape[2:], jnp.bfloat16),
            jax.ShapeDtypeStruct(resp_keys.shape[2:], jnp.bfloat16),
            jax.ShapeDtypeStruct(resp_values.shape[2:], jnp.bfloat16),
        ]
        + [jax.ShapeDtypeStruct((2,) + prefix_keys.shape[1:], jnp.bfloat16) for _ in range(n)]
        + [jax.ShapeDtypeStruct((1,), jnp.float32)],
    )(scalars, queries[0, 0], cotangent[0, 0], resp_keys[0, 0], resp_values[0, 0], *pieces)
    grad_q, grad_k, grad_v = results[:3]
    parts = results[3:-1]
    forget_loss = results[-1]
    if n == 4:
        relayed = shifted(parts[3], -1, n)
        merged = (parts[1].astype(jnp.float32) + relayed.astype(jnp.float32)).astype(jnp.bfloat16)
        returned = [parts[0], shifted(parts[2], 1, n), shifted(merged, -1, n)]
    else:
        returned = [parts[0]] + [shifted(parts[k], -k, n) for k in range(1, n)]
    summed_keys = sum(r[0].astype(jnp.float32) for r in returned).astype(jnp.bfloat16)
    summed_values = sum(r[1].astype(jnp.float32) for r in returned).astype(jnp.bfloat16)
    return (
        grad_q[None, None],
        grad_k[None, None],
        grad_v[None, None],
        summed_keys[None],
        summed_values[None],
        forget_loss,
    )


def solution(mesh):
    placed = (
        P(("groups", "prompt"), "resp", None, None),
        P(("groups", "prompt"), "resp", None, None),
        P(("groups", "prompt"), "resp", None, None),
        P(("groups", "prompt"), "resp", None, None),
        P(("groups", "prompt"), "resp", None),
        P(("groups", "prompt"), "resp", None),
        P(("groups", "prompt")),
        P(("groups", "prompt"), "resp"),
        P(("groups", "prompt"), "resp"),
        P(("groups", "prompt"), "resp"),
    )
    return jax.shard_map(
        on_device,
        mesh=mesh,
        in_specs=placed,
        out_specs=(
            P(("groups", "prompt"), "resp", None, None),
            P(("groups", "prompt"), "resp", None, None),
            P(("groups", "prompt"), "resp", None, None),
            P(("groups", "prompt"), "resp", None),
            P(("groups", "prompt"), "resp", None),
            P(("groups", "prompt")),
        ),
        check_vma=False,
    )
```

```python
import functools
import math

import jax
import jax.numpy as jnp
from jax import lax
from jax.experimental import pallas as pl
from jax.experimental.pallas import tpu as pltpu
from jax.sharding import PartitionSpec as P

HEADS = 64
KV_HEADS = 4
HEAD_DIM = 128


loss_beta = 0.5
masked_score = -1e30


def attention_kernel(n_pieces, scalar_ref, q_ref, cot_ref, kown_ref, vown_ref, *rest):
    piece_refs = rest[:n_pieces]
    dq_ref, dkown_ref, dvown_ref = rest[n_pieces:n_pieces + 3]
    part_refs = rest[n_pieces + 3:-1]
    loss_ref = rest[-1]
    group_size = HEADS // KV_HEADS
    resp_len = q_ref.shape[0]
    piece_len = part_refs[0].shape[1]
    scaling = 1.0 / math.sqrt(HEAD_DIM)
    rows = group_size * resp_len
    token = lax.broadcasted_iota(jnp.int32, (resp_len, 1), 0).astype(jnp.float32)
    factor = jnp.where(token < scalar_ref[1], scalar_ref[0], 0.0)

    @pl.when(pl.program_id(0) == 0)
    def _():
        term_total = scalar_ref[2]
        for r in piece_refs[1:]:
            term_total = term_total + jnp.sum(r[2 * piece_len:2 * piece_len + 8, :].astype(jnp.float32))
        loss_ref[0] = term_total / scalar_ref[3]
    contract_minor = (((1,), (1,)), ((), ()))
    contract_major = (((0,), (0,)), ((), ()))
    q_all = q_ref[...]
    g_all = (cot_ref[...].astype(jnp.float32) * factor).astype(jnp.bfloat16)
    q_rows = jnp.concatenate([q_all[:, h * HEAD_DIM:(h + 1) * HEAD_DIM] for h in range(group_size)], axis=0)
    g_rows = jnp.concatenate([g_all[:, h * HEAD_DIM:(h + 1) * HEAD_DIM] for h in range(group_size)], axis=0)
    k_pre = jnp.concatenate([r[:piece_len] for r in piece_refs], axis=0)
    v_pre = jnp.concatenate([r[piece_len:2 * piece_len] for r in piece_refs], axis=0)
    k_own = kown_ref[...]
    v_own = vown_ref[...]
    s_pre = lax.dot_general(k_pre, q_rows, contract_minor, preferred_element_type=jnp.float32)
    s_own = lax.dot_general(k_own, q_rows, contract_minor, preferred_element_type=jnp.float32)
    own_pos = lax.broadcasted_iota(jnp.int32, (resp_len, rows), 0)
    token_of_col = lax.broadcasted_iota(jnp.int32, (resp_len, rows), 1) % resp_len
    s_own = jnp.where(token_of_col >= own_pos, s_own, masked_score)
    peak = jnp.maximum(jnp.max(s_pre, axis=0, keepdims=True), jnp.max(s_own, axis=0, keepdims=True))
    exp_scale = scaling * math.log2(math.e)
    e_pre = jnp.exp2((s_pre - peak) * exp_scale)
    e_own = jnp.exp2((s_own - peak) * exp_scale)
    total = jnp.sum(e_pre, axis=0, keepdims=True) + jnp.sum(e_own, axis=0, keepdims=True)
    inv_total = 1.0 / total
    p_pre = e_pre * inv_total
    p_own = e_own * inv_total
    dp_pre = lax.dot_general(v_pre, g_rows, contract_minor, preferred_element_type=jnp.float32)
    dp_own = lax.dot_general(v_own, g_rows, contract_minor, preferred_element_type=jnp.float32)
    centre = jnp.sum(p_pre * dp_pre, axis=0, keepdims=True) + jnp.sum(p_own * dp_own, axis=0, keepdims=True)
    ds_pre = (p_pre * (dp_pre - centre)).astype(jnp.bfloat16)
    ds_own = (p_own * (dp_own - centre)).astype(jnp.bfloat16)
    dk_pre = jnp.dot(ds_pre, q_rows, preferred_element_type=jnp.float32) * scaling
    dv_pre = jnp.dot(p_pre.astype(jnp.bfloat16), g_rows, preferred_element_type=jnp.float32)
    for i, r in enumerate(part_refs):
        r[0] = dk_pre[i * piece_len:(i + 1) * piece_len].astype(jnp.bfloat16)
        r[1] = dv_pre[i * piece_len:(i + 1) * piece_len].astype(jnp.bfloat16)
    dkown_ref[...] = (jnp.dot(ds_own, q_rows, preferred_element_type=jnp.float32) * scaling).astype(jnp.bfloat16)
    dvown_ref[...] = jnp.dot(p_own.astype(jnp.bfloat16), g_rows, preferred_element_type=jnp.float32).astype(
        jnp.bfloat16
    )
    dq_rows = (
        lax.dot_general(ds_pre, k_pre, contract_major, preferred_element_type=jnp.float32) * scaling
        + lax.dot_general(ds_own, k_own, contract_major, preferred_element_type=jnp.float32) * scaling
    )
    for h in range(group_size):
        dq_ref[:, h * HEAD_DIM:(h + 1) * HEAD_DIM] = dq_rows[h * resp_len:(h + 1) * resp_len].astype(jnp.bfloat16)


def split_words(value):
    high = value.astype(jnp.bfloat16)
    rest = value - high.astype(jnp.float32)
    middle = rest.astype(jnp.bfloat16)
    low = (rest - middle.astype(jnp.float32)).astype(jnp.bfloat16)
    return jnp.stack([high, middle, low])


def shifted(value, shift, n):
    return lax.ppermute(value, "resp", [(i, (i + shift) % n) for i in range(n)])


def on_device(
    queries,
    cotangent,
    resp_keys,
    resp_values,
    prefix_keys,
    prefix_values,
    counts,
    lengths,
    policy_likelihood,
    reference_likelihood,
):
    n = lax.axis_size("resp")
    slot_count = queries.shape[1]
    assert slot_count == 1
    resp_len = queries.shape[2]
    piece_len = prefix_keys.shape[1]
    live_count = counts[0]
    count_real = live_count.astype(jnp.float32)
    slot_ids = lax.axis_index("resp") * slot_count + jnp.arange(slot_count, dtype=jnp.int32)
    live_slots = slot_ids < live_count
    margin = policy_likelihood[0] - reference_likelihood[0]
    weight = jnp.where(live_slots, 2.0 * jax.nn.sigmoid(loss_beta * margin) / count_real, 0.0)
    loss_terms = jnp.where(live_slots, 2.0 / loss_beta * jax.nn.softplus(loss_beta * margin), 0.0)
    own_term = jnp.sum(loss_terms)
    word_rows = jnp.zeros((16, prefix_keys.shape[2]), jnp.bfloat16)
    word_rows = word_rows.at[0, 0:3].set(split_words(own_term))
    local_kv = jnp.concatenate([prefix_keys[0], prefix_values[0], word_rows], axis=0)
    if n == 4:
        from_left = shifted(local_kv, 1, n)
        pieces = [local_kv, from_left, shifted(local_kv, -1, n), shifted(from_left, 1, n)]
    else:
        pieces = [local_kv] + [shifted(local_kv, k, n) for k in range(1, n)]
    scalars = jnp.stack([weight[0], lengths[0][0].astype(jnp.float32), own_term, count_real])
    group_width = (HEADS // KV_HEADS) * HEAD_DIM
    piece_block = pl.BlockSpec((2 * piece_len + 16, HEAD_DIM), lambda g: (0, g))
    part_block = pl.BlockSpec((2, piece_len, HEAD_DIM), lambda g: (0, 0, g))
    results = pl.pallas_call(
        functools.partial(attention_kernel, n),
        grid=(KV_HEADS,),
        in_specs=[
            pl.BlockSpec(memory_space=pltpu.SMEM),
            pl.BlockSpec((resp_len, group_width), lambda g: (0, g)),
            pl.BlockSpec((resp_len, group_width), lambda g: (0, g)),
            pl.BlockSpec((resp_len, HEAD_DIM), lambda g: (0, g)),
            pl.BlockSpec((resp_len, HEAD_DIM), lambda g: (0, g)),
        ]
        + [piece_block] * n,
        out_specs=[
            pl.BlockSpec((resp_len, group_width), lambda g: (0, g)),
            pl.BlockSpec((resp_len, HEAD_DIM), lambda g: (0, g)),
            pl.BlockSpec((resp_len, HEAD_DIM), lambda g: (0, g)),
        ]
        + [part_block] * n
        + [pl.BlockSpec(memory_space=pltpu.SMEM)],
        out_shape=[
            jax.ShapeDtypeStruct(queries.shape[2:], jnp.bfloat16),
            jax.ShapeDtypeStruct(resp_keys.shape[2:], jnp.bfloat16),
            jax.ShapeDtypeStruct(resp_values.shape[2:], jnp.bfloat16),
        ]
        + [jax.ShapeDtypeStruct((2,) + prefix_keys.shape[1:], jnp.bfloat16) for _ in range(n)]
        + [jax.ShapeDtypeStruct((1,), jnp.float32)],
    )(scalars, queries[0, 0], cotangent[0, 0], resp_keys[0, 0], resp_values[0, 0], *pieces)
    grad_q, grad_k, grad_v = results[:3]
    parts = results[3:-1]
    forget_loss = results[-1]
    if n == 4:
        relayed = shifted(parts[3], -1, n)
        merged = (parts[1].astype(jnp.float32) + relayed.astype(jnp.float32)).astype(jnp.bfloat16)
        returned = [parts[0], shifted(parts[2], 1, n), shifted(merged, -1, n)]
    else:
        returned = [parts[0]] + [shifted(parts[k], -k, n) for k in range(1, n)]
    summed_keys = sum(r[0].astype(jnp.float32) for r in returned).astype(jnp.bfloat16)
    summed_values = sum(r[1].astype(jnp.float32) for r in returned).astype(jnp.bfloat16)
    return (
        grad_q[None, None],
        grad_k[None, None],
        grad_v[None, None],
        summed_keys[None],
        summed_values[None],
        forget_loss,
    )


def solution(mesh):
    placed = (
        P(("groups", "prompt"), "resp", None, None),
        P(("groups", "prompt"), "resp", None, None),
        P(("groups", "prompt"), "resp", None, None),
        P(("groups", "prompt"), "resp", None, None),
        P(("groups", "prompt"), "resp", None),
        P(("groups", "prompt"), "resp", None),
        P(("groups", "prompt")),
        P(("groups", "prompt"), "resp"),
        P(("groups", "prompt"), "resp"),
        P(("groups", "prompt"), "resp"),
    )
    return jax.shard_map(
        on_device,
        mesh=mesh,
        in_specs=placed,
        out_specs=(
            P(("groups", "prompt"), "resp", None, None),
            P(("groups", "prompt"), "resp", None, None),
            P(("groups", "prompt"), "resp", None, None),
            P(("groups", "prompt"), "resp", None),
            P(("groups", "prompt"), "resp", None),
            P(("groups", "prompt")),
        ),
        check_vma=False,
    )
```

```python
import functools
import math

import jax
import jax.numpy as jnp
from jax import lax
from jax.experimental import pallas as pl
from jax.experimental.pallas import tpu as pltpu
from jax.sharding import PartitionSpec as P

HEADS = 64
KV_HEADS = 4
HEAD_DIM = 128


loss_beta = 0.5
masked_score = -1e30


def attention_kernel(n_pieces, scalar_ref, q_ref, cot_ref, kown_ref, vown_ref, *rest):
    piece_refs = rest[:n_pieces]
    dq_ref, dkown_ref, dvown_ref = rest[n_pieces:n_pieces + 3]
    part_refs = rest[n_pieces + 3:2 * n_pieces + 3]
    loss_ref = rest[2 * n_pieces + 3]
    s_ref, dp_ref, e_ref, ds_ref, pb_ref = rest[2 * n_pieces + 4:]
    group_size = HEADS // KV_HEADS
    resp_len = q_ref.shape[0]
    piece_len = part_refs[0].shape[1]
    prefix_rows = n_pieces * piece_len
    all_rows = prefix_rows + resp_len
    scaling = 1.0 / math.sqrt(HEAD_DIM)
    exp_scale = scaling * math.log2(math.e)
    rows = group_size * resp_len
    chunk = 32
    chunks = prefix_rows // chunk
    token = lax.broadcasted_iota(jnp.int32, (resp_len, 1), 0).astype(jnp.float32)
    factor = jnp.where(token < scalar_ref[1], scalar_ref[0], 0.0)

    @pl.when(pl.program_id(0) == 0)
    def _():
        term_total = scalar_ref[2]
        for r in piece_refs[1:]:
            term_total = term_total + jnp.sum(r[2 * piece_len:2 * piece_len + 8, :].astype(jnp.float32))
        loss_ref[0] = term_total / scalar_ref[3]

    contract_minor = (((1,), (1,)), ((), ()))
    contract_major = (((0,), (0,)), ((), ()))
    q_all = q_ref[...]
    g_all = (cot_ref[...].astype(jnp.float32) * factor).astype(jnp.bfloat16)
    q_rows = jnp.concatenate([q_all[:, h * HEAD_DIM:(h + 1) * HEAD_DIM] for h in range(group_size)], axis=0)
    g_rows = jnp.concatenate([g_all[:, h * HEAD_DIM:(h + 1) * HEAD_DIM] for h in range(group_size)], axis=0)
    k_all = jnp.concatenate([r[:piece_len] for r in piece_refs] + [kown_ref[...]], axis=0)
    v_all = jnp.concatenate([r[piece_len:2 * piece_len] for r in piece_refs] + [vown_ref[...]], axis=0)
    s_ref[...] = lax.dot_general(k_all, q_rows, contract_minor, preferred_element_type=jnp.float32)
    dp_ref[...] = lax.dot_general(v_all, g_rows, contract_minor, preferred_element_type=jnp.float32)
    own_pos = lax.broadcasted_iota(jnp.int32, (resp_len, rows), 0)
    token_of_col = lax.broadcasted_iota(jnp.int32, (resp_len, rows), 1) % resp_len
    s_own = jnp.where(token_of_col >= own_pos, s_ref[prefix_rows:all_rows], masked_score)

    def block(c):
        return pl.ds(pl.multiple_of(c * chunk, chunk), chunk)

    def max_step(c, running):
        return jnp.maximum(running, s_ref[block(c)])

    running = lax.fori_loop(0, chunks, max_step, jnp.full((chunk, rows), masked_score, jnp.float32), unroll=True)
    peak = jnp.maximum(jnp.max(running, axis=0, keepdims=True), jnp.max(s_own, axis=0, keepdims=True))

    def exp_step(c, running):
        e = jnp.exp2((s_ref[block(c)] - peak) * exp_scale)
        e_ref[block(c)] = e
        return running + e

    running = lax.fori_loop(0, chunks, exp_step, jnp.zeros((chunk, rows), jnp.float32), unroll=True)
    e_own = jnp.exp2((s_own - peak) * exp_scale)
    e_ref[prefix_rows:all_rows] = e_own
    total = jnp.sum(running, axis=0, keepdims=True) + jnp.sum(e_own, axis=0, keepdims=True)
    inv_total = 1.0 / total

    def centre_step(c, running):
        return running + (e_ref[block(c)] * inv_total) * dp_ref[block(c)]

    running = lax.fori_loop(0, chunks, centre_step, jnp.zeros((chunk, rows), jnp.float32), unroll=True)
    p_own = e_own * inv_total
    centre = jnp.sum(running, axis=0, keepdims=True) + jnp.sum(
        p_own * dp_ref[prefix_rows:all_rows], axis=0, keepdims=True
    )

    def shift_step(c, carry):
        p = e_ref[block(c)] * inv_total
        ds_ref[block(c)] = (p * (dp_ref[block(c)] - centre)).astype(jnp.bfloat16)
        pb_ref[block(c)] = p.astype(jnp.bfloat16)
        return carry

    lax.fori_loop(0, chunks, shift_step, 0, unroll=True)
    ds_ref[prefix_rows:all_rows] = (p_own * (dp_ref[prefix_rows:all_rows] - centre)).astype(jnp.bfloat16)
    pb_ref[prefix_rows:all_rows] = p_own.astype(jnp.bfloat16)
    ds_all = ds_ref[...]
    dk_all = jnp.dot(ds_all, q_rows, preferred_element_type=jnp.float32) * scaling
    dv_all = jnp.dot(pb_ref[...], g_rows, preferred_element_type=jnp.float32)
    for i, r in enumerate(part_refs):
        r[0] = dk_all[i * piece_len:(i + 1) * piece_len].astype(jnp.bfloat16)
        r[1] = dv_all[i * piece_len:(i + 1) * piece_len].astype(jnp.bfloat16)
    dkown_ref[...] = dk_all[prefix_rows:all_rows].astype(jnp.bfloat16)
    dvown_ref[...] = dv_all[prefix_rows:all_rows].astype(jnp.bfloat16)
    dq_rows = lax.dot_general(ds_all, k_all, contract_major, preferred_element_type=jnp.float32) * scaling
    for h in range(group_size):
        dq_ref[:, h * HEAD_DIM:(h + 1) * HEAD_DIM] = dq_rows[h * resp_len:(h + 1) * resp_len].astype(jnp.bfloat16)


def split_words(value):
    high = value.astype(jnp.bfloat16)
    rest = value - high.astype(jnp.float32)
    middle = rest.astype(jnp.bfloat16)
    low = (rest - middle.astype(jnp.float32)).astype(jnp.bfloat16)
    return jnp.stack([high, middle, low])


def shifted(value, shift, n):
    return lax.ppermute(value, "resp", [(i, (i + shift) % n) for i in range(n)])


def on_device(
    queries,
    cotangent,
    resp_keys,
    resp_values,
    prefix_keys,
    prefix_values,
    counts,
    lengths,
    policy_likelihood,
    reference_likelihood,
):
    n = lax.axis_size("resp")
    slot_count = queries.shape[1]
    assert slot_count == 1
    resp_len = queries.shape[2]
    piece_len = prefix_keys.shape[1]
    live_count = counts[0]
    count_real = live_count.astype(jnp.float32)
    slot_ids = lax.axis_index("resp") * slot_count + jnp.arange(slot_count, dtype=jnp.int32)
    live_slots = slot_ids < live_count
    margin = policy_likelihood[0] - reference_likelihood[0]
    weight = jnp.where(live_slots, 2.0 * jax.nn.sigmoid(loss_beta * margin) / count_real, 0.0)
    loss_terms = jnp.where(live_slots, 2.0 / loss_beta * jax.nn.softplus(loss_beta * margin), 0.0)
    own_term = jnp.sum(loss_terms)
    word_rows = jnp.zeros((16, prefix_keys.shape[2]), jnp.bfloat16)
    word_rows = word_rows.at[0, 0:3].set(split_words(own_term))
    local_kv = jnp.concatenate([prefix_keys[0], prefix_values[0], word_rows], axis=0)
    if n == 4:
        from_left = shifted(local_kv, 1, n)
        pieces = [local_kv, from_left, shifted(local_kv, -1, n), shifted(from_left, 1, n)]
    else:
        pieces = [local_kv] + [shifted(local_kv, k, n) for k in range(1, n)]
    scalars = jnp.stack([weight[0], lengths[0][0].astype(jnp.float32), own_term, count_real])
    group_width = (HEADS // KV_HEADS) * HEAD_DIM
    group_rows = (HEADS // KV_HEADS) * resp_len
    all_rows = n * piece_len + resp_len
    piece_block = pl.BlockSpec((2 * piece_len + 16, HEAD_DIM), lambda g: (0, g))
    part_block = pl.BlockSpec((2, piece_len, HEAD_DIM), lambda g: (0, 0, g))
    results = pl.pallas_call(
        functools.partial(attention_kernel, n),
        grid=(KV_HEADS,),
        in_specs=[
            pl.BlockSpec(memory_space=pltpu.SMEM),
            pl.BlockSpec((resp_len, group_width), lambda g: (0, g)),
            pl.BlockSpec((resp_len, group_width), lambda g: (0, g)),
            pl.BlockSpec((resp_len, HEAD_DIM), lambda g: (0, g)),
            pl.BlockSpec((resp_len, HEAD_DIM), lambda g: (0, g)),
        ]
        + [piece_block] * n,
        out_specs=[
            pl.BlockSpec((resp_len, group_width), lambda g: (0, g)),
            pl.BlockSpec((resp_len, HEAD_DIM), lambda g: (0, g)),
            pl.BlockSpec((resp_len, HEAD_DIM), lambda g: (0, g)),
        ]
        + [part_block] * n
        + [pl.BlockSpec(memory_space=pltpu.SMEM)],
        out_shape=[
            jax.ShapeDtypeStruct(queries.shape[2:], jnp.bfloat16),
            jax.ShapeDtypeStruct(resp_keys.shape[2:], jnp.bfloat16),
            jax.ShapeDtypeStruct(resp_values.shape[2:], jnp.bfloat16),
        ]
        + [jax.ShapeDtypeStruct((2,) + prefix_keys.shape[1:], jnp.bfloat16) for _ in range(n)]
        + [jax.ShapeDtypeStruct((1,), jnp.float32)],
        scratch_shapes=[pltpu.VMEM((all_rows, group_rows), jnp.float32) for _ in range(3)]
        + [pltpu.VMEM((all_rows, group_rows), jnp.bfloat16) for _ in range(2)],
        compiler_params=pltpu.CompilerParams(vmem_limit_bytes=48 * 1024 * 1024),
    )(scalars, queries[0, 0], cotangent[0, 0], resp_keys[0, 0], resp_values[0, 0], *pieces)
    grad_q, grad_k, grad_v = results[:3]
    parts = results[3:-1]
    forget_loss = results[-1]
    if n == 4:
        relayed = shifted(parts[3], -1, n)
        merged = (parts[1].astype(jnp.float32) + relayed.astype(jnp.float32)).astype(jnp.bfloat16)
        returned = [parts[0], shifted(parts[2], 1, n), shifted(merged, -1, n)]
    else:
        returned = [parts[0]] + [shifted(parts[k], -k, n) for k in range(1, n)]
    summed_keys = sum(r[0].astype(jnp.float32) for r in returned).astype(jnp.bfloat16)
    summed_values = sum(r[1].astype(jnp.float32) for r in returned).astype(jnp.bfloat16)
    return (
        grad_q[None, None],
        grad_k[None, None],
        grad_v[None, None],
        summed_keys[None],
        summed_values[None],
        forget_loss,
    )


def solution(mesh):
    placed = (
        P(("groups", "prompt"), "resp", None, None),
        P(("groups", "prompt"), "resp", None, None),
        P(("groups", "prompt"), "resp", None, None),
        P(("groups", "prompt"), "resp", None, None),
        P(("groups", "prompt"), "resp", None),
        P(("groups", "prompt"), "resp", None),
        P(("groups", "prompt")),
        P(("groups", "prompt"), "resp"),
        P(("groups", "prompt"), "resp"),
        P(("groups", "prompt"), "resp"),
    )
    return jax.shard_map(
        on_device,
        mesh=mesh,
        in_specs=placed,
        out_specs=(
            P(("groups", "prompt"), "resp", None, None),
            P(("groups", "prompt"), "resp", None, None),
            P(("groups", "prompt"), "resp", None, None),
            P(("groups", "prompt"), "resp", None),
            P(("groups", "prompt"), "resp", None),
            P(("groups", "prompt")),
        ),
        check_vma=False,
    )
```

```python
import functools
import math

import jax
import jax.numpy as jnp
from jax import lax
from jax.experimental import pallas as pl
from jax.experimental.pallas import tpu as pltpu
from jax.sharding import PartitionSpec as P

HEADS = 64
KV_HEADS = 4
HEAD_DIM = 128


loss_beta = 0.5
masked_score = -1e30


def attention_kernel(n_pieces, scalar_ref, q_ref, cot_ref, kown_ref, vown_ref, *rest):
    piece_refs = rest[:n_pieces]
    dq_ref, dkown_ref, dvown_ref = rest[n_pieces:n_pieces + 3]
    part_refs = rest[n_pieces + 3:2 * n_pieces + 3]
    loss_ref = rest[2 * n_pieces + 3]
    s_ref, dp_ref, e_ref, ds_ref, pb_ref = rest[2 * n_pieces + 4:]
    group_size = HEADS // KV_HEADS
    resp_len = q_ref.shape[0]
    piece_len = part_refs[0].shape[1]
    prefix_rows = n_pieces * piece_len
    all_rows = prefix_rows + resp_len
    scaling = 1.0 / math.sqrt(HEAD_DIM)
    exp_scale = scaling * math.log2(math.e)
    rows = group_size * resp_len
    chunk = 32
    chunks = prefix_rows // chunk
    token = lax.broadcasted_iota(jnp.int32, (resp_len, 1), 0).astype(jnp.float32)
    factor = jnp.where(token < scalar_ref[1], scalar_ref[0], 0.0)

    @pl.when(pl.program_id(0) == 0)
    def _():
        term_total = scalar_ref[2]
        for r in piece_refs[1:]:
            term_total = term_total + jnp.sum(r[2 * piece_len:2 * piece_len + 8, :].astype(jnp.float32))
        loss_ref[0] = term_total / scalar_ref[3]

    contract_minor = (((1,), (1,)), ((), ()))
    contract_major = (((0,), (0,)), ((), ()))
    q_all = q_ref[...]
    g_all = (cot_ref[...].astype(jnp.float32) * factor).astype(jnp.bfloat16)
    q_rows = jnp.concatenate([q_all[:, h * HEAD_DIM:(h + 1) * HEAD_DIM] for h in range(group_size)], axis=0)
    g_rows = jnp.concatenate([g_all[:, h * HEAD_DIM:(h + 1) * HEAD_DIM] for h in range(group_size)], axis=0)
    cols = pl.ds(pl.multiple_of(pl.program_id(0) * HEAD_DIM, HEAD_DIM), HEAD_DIM)
    k_all = jnp.concatenate([r[:piece_len, cols] for r in piece_refs] + [kown_ref[...]], axis=0)
    v_all = jnp.concatenate([r[piece_len:2 * piece_len, cols] for r in piece_refs] + [vown_ref[...]], axis=0)
    s_ref[...] = lax.dot_general(k_all, q_rows, contract_minor, preferred_element_type=jnp.float32)
    dp_ref[...] = lax.dot_general(v_all, g_rows, contract_minor, preferred_element_type=jnp.float32)
    own_pos = lax.broadcasted_iota(jnp.int32, (resp_len, rows), 0)
    token_of_col = lax.broadcasted_iota(jnp.int32, (resp_len, rows), 1) % resp_len
    s_own = jnp.where(token_of_col >= own_pos, s_ref[prefix_rows:all_rows], masked_score)

    def block(c):
        return pl.ds(pl.multiple_of(c * chunk, chunk), chunk)

    def max_step(c, running):
        return jnp.maximum(running, s_ref[block(c)])

    running = lax.fori_loop(0, chunks, max_step, jnp.full((chunk, rows), masked_score, jnp.float32), unroll=True)
    peak = jnp.maximum(jnp.max(running, axis=0, keepdims=True), jnp.max(s_own, axis=0, keepdims=True))

    def exp_step(c, running):
        e = jnp.exp2((s_ref[block(c)] - peak) * exp_scale)
        e_ref[block(c)] = e
        return running + e

    running = lax.fori_loop(0, chunks, exp_step, jnp.zeros((chunk, rows), jnp.float32), unroll=True)
    e_own = jnp.exp2((s_own - peak) * exp_scale)
    e_ref[prefix_rows:all_rows] = e_own
    total = jnp.sum(running, axis=0, keepdims=True) + jnp.sum(e_own, axis=0, keepdims=True)
    inv_total = 1.0 / total

    def centre_step(c, running):
        return running + (e_ref[block(c)] * inv_total) * dp_ref[block(c)]

    running = lax.fori_loop(0, chunks, centre_step, jnp.zeros((chunk, rows), jnp.float32), unroll=True)
    p_own = e_own * inv_total
    centre = jnp.sum(running, axis=0, keepdims=True) + jnp.sum(
        p_own * dp_ref[prefix_rows:all_rows], axis=0, keepdims=True
    )

    def shift_step(c, carry):
        p = e_ref[block(c)] * inv_total
        ds_ref[block(c)] = (p * (dp_ref[block(c)] - centre)).astype(jnp.bfloat16)
        pb_ref[block(c)] = p.astype(jnp.bfloat16)
        return carry

    lax.fori_loop(0, chunks, shift_step, 0, unroll=True)
    ds_ref[prefix_rows:all_rows] = (p_own * (dp_ref[prefix_rows:all_rows] - centre)).astype(jnp.bfloat16)
    pb_ref[prefix_rows:all_rows] = p_own.astype(jnp.bfloat16)
    ds_all = ds_ref[...]
    dk_all = jnp.dot(ds_all, q_rows, preferred_element_type=jnp.float32) * scaling
    dv_all = jnp.dot(pb_ref[...], g_rows, preferred_element_type=jnp.float32)
    for i, r in enumerate(part_refs):
        r[0, :, cols] = dk_all[i * piece_len:(i + 1) * piece_len].astype(jnp.bfloat16)
        r[1, :, cols] = dv_all[i * piece_len:(i + 1) * piece_len].astype(jnp.bfloat16)
    dkown_ref[...] = dk_all[prefix_rows:all_rows].astype(jnp.bfloat16)
    dvown_ref[...] = dv_all[prefix_rows:all_rows].astype(jnp.bfloat16)
    dq_rows = lax.dot_general(ds_all, k_all, contract_major, preferred_element_type=jnp.float32) * scaling
    for h in range(group_size):
        dq_ref[:, h * HEAD_DIM:(h + 1) * HEAD_DIM] = dq_rows[h * resp_len:(h + 1) * resp_len].astype(jnp.bfloat16)


def split_words(value):
    high = value.astype(jnp.bfloat16)
    rest = value - high.astype(jnp.float32)
    middle = rest.astype(jnp.bfloat16)
    low = (rest - middle.astype(jnp.float32)).astype(jnp.bfloat16)
    return jnp.stack([high, middle, low])


def shifted(value, shift, n):
    return lax.ppermute(value, "resp", [(i, (i + shift) % n) for i in range(n)])


def on_device(
    queries,
    cotangent,
    resp_keys,
    resp_values,
    prefix_keys,
    prefix_values,
    counts,
    lengths,
    policy_likelihood,
    reference_likelihood,
):
    n = lax.axis_size("resp")
    slot_count = queries.shape[1]
    assert slot_count == 1
    resp_len = queries.shape[2]
    piece_len = prefix_keys.shape[1]
    live_count = counts[0]
    count_real = live_count.astype(jnp.float32)
    slot_ids = lax.axis_index("resp") * slot_count + jnp.arange(slot_count, dtype=jnp.int32)
    live_slots = slot_ids < live_count
    margin = policy_likelihood[0] - reference_likelihood[0]
    weight = jnp.where(live_slots, 2.0 * jax.nn.sigmoid(loss_beta * margin) / count_real, 0.0)
    loss_terms = jnp.where(live_slots, 2.0 / loss_beta * jax.nn.softplus(loss_beta * margin), 0.0)
    own_term = jnp.sum(loss_terms)
    word_rows = jnp.zeros((16, prefix_keys.shape[2]), jnp.bfloat16)
    word_rows = word_rows.at[0, 0:3].set(split_words(own_term))
    local_kv = jnp.concatenate([prefix_keys[0], prefix_values[0], word_rows], axis=0)
    if n == 4:
        from_left = shifted(local_kv, 1, n)
        pieces = [local_kv, from_left, shifted(local_kv, -1, n), shifted(from_left, 1, n)]
    else:
        pieces = [local_kv] + [shifted(local_kv, k, n) for k in range(1, n)]
    scalars = jnp.stack([weight[0], lengths[0][0].astype(jnp.float32), own_term, count_real])
    group_width = (HEADS // KV_HEADS) * HEAD_DIM
    group_rows = (HEADS // KV_HEADS) * resp_len
    all_rows = n * piece_len + resp_len
    piece_block = pl.BlockSpec(memory_space=pltpu.VMEM)
    part_block = pl.BlockSpec(memory_space=pltpu.VMEM)
    results = pl.pallas_call(
        functools.partial(attention_kernel, n),
        grid=(KV_HEADS,),
        in_specs=[
            pl.BlockSpec(memory_space=pltpu.SMEM),
            pl.BlockSpec((resp_len, group_width), lambda g: (0, g)),
            pl.BlockSpec((resp_len, group_width), lambda g: (0, g)),
            pl.BlockSpec((resp_len, HEAD_DIM), lambda g: (0, g)),
            pl.BlockSpec((resp_len, HEAD_DIM), lambda g: (0, g)),
        ]
        + [piece_block] * n,
        out_specs=[
            pl.BlockSpec((resp_len, group_width), lambda g: (0, g)),
            pl.BlockSpec((resp_len, HEAD_DIM), lambda g: (0, g)),
            pl.BlockSpec((resp_len, HEAD_DIM), lambda g: (0, g)),
        ]
        + [part_block] * n
        + [pl.BlockSpec(memory_space=pltpu.SMEM)],
        out_shape=[
            jax.ShapeDtypeStruct(queries.shape[2:], jnp.bfloat16),
            jax.ShapeDtypeStruct(resp_keys.shape[2:], jnp.bfloat16),
            jax.ShapeDtypeStruct(resp_values.shape[2:], jnp.bfloat16),
        ]
        + [jax.ShapeDtypeStruct((2,) + prefix_keys.shape[1:], jnp.bfloat16) for _ in range(n)]
        + [jax.ShapeDtypeStruct((1,), jnp.float32)],
        scratch_shapes=[pltpu.VMEM((all_rows, group_rows), jnp.float32) for _ in range(3)]
        + [pltpu.VMEM((all_rows, group_rows), jnp.bfloat16) for _ in range(2)],
        compiler_params=pltpu.CompilerParams(vmem_limit_bytes=48 * 1024 * 1024),
    )(scalars, queries[0, 0], cotangent[0, 0], resp_keys[0, 0], resp_values[0, 0], *pieces)
    grad_q, grad_k, grad_v = results[:3]
    parts = results[3:-1]
    forget_loss = results[-1]
    if n == 4:
        relayed = shifted(parts[3], -1, n)
        merged = (parts[1].astype(jnp.float32) + relayed.astype(jnp.float32)).astype(jnp.bfloat16)
        returned = [parts[0], shifted(parts[2], 1, n), shifted(merged, -1, n)]
    else:
        returned = [parts[0]] + [shifted(parts[k], -k, n) for k in range(1, n)]
    summed_keys = sum(r[0].astype(jnp.float32) for r in returned).astype(jnp.bfloat16)
    summed_values = sum(r[1].astype(jnp.float32) for r in returned).astype(jnp.bfloat16)
    return (
        grad_q[None, None],
        grad_k[None, None],
        grad_v[None, None],
        summed_keys[None],
        summed_values[None],
        forget_loss,
    )


def solution(mesh):
    placed = (
        P(("groups", "prompt"), "resp", None, None),
        P(("groups", "prompt"), "resp", None, None),
        P(("groups", "prompt"), "resp", None, None),
        P(("groups", "prompt"), "resp", None, None),
        P(("groups", "prompt"), "resp", None),
        P(("groups", "prompt"), "resp", None),
        P(("groups", "prompt")),
        P(("groups", "prompt"), "resp"),
        P(("groups", "prompt"), "resp"),
        P(("groups", "prompt"), "resp"),
    )
    return jax.shard_map(
        on_device,
        mesh=mesh,
        in_specs=placed,
        out_specs=(
            P(("groups", "prompt"), "resp", None, None),
            P(("groups", "prompt"), "resp", None, None),
            P(("groups", "prompt"), "resp", None, None),
            P(("groups", "prompt"), "resp", None),
            P(("groups", "prompt"), "resp", None),
            P(("groups", "prompt")),
        ),
        check_vma=False,
    )
```

```python
import functools
import math

import jax
import jax.numpy as jnp
from jax import lax
from jax.experimental import pallas as pl
from jax.experimental.pallas import tpu as pltpu
from jax.sharding import PartitionSpec as P

HEADS = 64
KV_HEADS = 4
HEAD_DIM = 128


loss_beta = 0.5
masked_score = -1e30


def attention_kernel(n_pieces, scalar_ref, q_ref, cot_ref, kown_ref, vown_ref, *rest):
    piece_refs = rest[:n_pieces]
    dq_ref, dkown_ref, dvown_ref = rest[n_pieces:n_pieces + 3]
    part_refs = rest[n_pieces + 3:2 * n_pieces + 3]
    loss_ref = rest[2 * n_pieces + 3]
    s_ref, dp_ref, e_ref, ds_ref, pb_ref = rest[2 * n_pieces + 4:]
    group_size = HEADS // KV_HEADS
    resp_len = q_ref.shape[0]
    piece_len = part_refs[0].shape[1]
    prefix_rows = n_pieces * piece_len
    all_rows = prefix_rows + resp_len
    scaling = 1.0 / math.sqrt(HEAD_DIM)
    exp_scale = scaling * math.log2(math.e)
    rows = group_size * resp_len
    chunk = 32
    chunks = prefix_rows // chunk
    token = lax.broadcasted_iota(jnp.int32, (resp_len, 1), 0).astype(jnp.float32)
    factor = jnp.where(token < scalar_ref[1], scalar_ref[0], 0.0)

    @pl.when(pl.program_id(0) == 0)
    def _():
        term_total = scalar_ref[2]
        for r in piece_refs[1:]:
            term_total = term_total + jnp.sum(r[2 * piece_len:2 * piece_len + 8, :].astype(jnp.float32))
        loss_ref[0] = term_total / scalar_ref[3]

    contract_minor = (((1,), (1,)), ((), ()))
    contract_major = (((0,), (0,)), ((), ()))
    group_cols = pl.ds(pl.multiple_of(pl.program_id(0) * rows * HEAD_DIM // resp_len, HEAD_DIM), rows * HEAD_DIM // resp_len)
    q_all = q_ref[:, group_cols]
    g_all = (cot_ref[:, group_cols].astype(jnp.float32) * factor).astype(jnp.bfloat16)
    q_rows = jnp.concatenate([q_all[:, h * HEAD_DIM:(h + 1) * HEAD_DIM] for h in range(group_size)], axis=0)
    g_rows = jnp.concatenate([g_all[:, h * HEAD_DIM:(h + 1) * HEAD_DIM] for h in range(group_size)], axis=0)
    cols = pl.ds(pl.multiple_of(pl.program_id(0) * HEAD_DIM, HEAD_DIM), HEAD_DIM)
    k_all = jnp.concatenate([r[:piece_len, cols] for r in piece_refs] + [kown_ref[...]], axis=0)
    v_all = jnp.concatenate([r[piece_len:2 * piece_len, cols] for r in piece_refs] + [vown_ref[...]], axis=0)
    s_ref[...] = lax.dot_general(k_all, q_rows, contract_minor, preferred_element_type=jnp.float32)
    dp_ref[...] = lax.dot_general(v_all, g_rows, contract_minor, preferred_element_type=jnp.float32)
    own_pos = lax.broadcasted_iota(jnp.int32, (resp_len, rows), 0)
    token_of_col = lax.broadcasted_iota(jnp.int32, (resp_len, rows), 1) % resp_len
    s_own = jnp.where(token_of_col >= own_pos, s_ref[prefix_rows:all_rows], masked_score)

    def block(c):
        return pl.ds(pl.multiple_of(c * chunk, chunk), chunk)

    def max_step(c, running):
        return jnp.maximum(running, s_ref[block(c)])

    running = lax.fori_loop(0, chunks, max_step, jnp.full((chunk, rows), masked_score, jnp.float32), unroll=True)
    peak = jnp.maximum(jnp.max(running, axis=0, keepdims=True), jnp.max(s_own, axis=0, keepdims=True))

    def exp_step(c, running):
        e = jnp.exp2((s_ref[block(c)] - peak) * exp_scale)
        e_ref[block(c)] = e
        return running + e

    running = lax.fori_loop(0, chunks, exp_step, jnp.zeros((chunk, rows), jnp.float32), unroll=True)
    e_own = jnp.exp2((s_own - peak) * exp_scale)
    e_ref[prefix_rows:all_rows] = e_own
    total = jnp.sum(running, axis=0, keepdims=True) + jnp.sum(e_own, axis=0, keepdims=True)
    inv_total = 1.0 / total

    def centre_step(c, running):
        return running + (e_ref[block(c)] * inv_total) * dp_ref[block(c)]

    running = lax.fori_loop(0, chunks, centre_step, jnp.zeros((chunk, rows), jnp.float32), unroll=True)
    p_own = e_own * inv_total
    centre = jnp.sum(running, axis=0, keepdims=True) + jnp.sum(
        p_own * dp_ref[prefix_rows:all_rows], axis=0, keepdims=True
    )

    def shift_step(c, carry):
        p = e_ref[block(c)] * inv_total
        ds_ref[block(c)] = (p * (dp_ref[block(c)] - centre)).astype(jnp.bfloat16)
        pb_ref[block(c)] = p.astype(jnp.bfloat16)
        return carry

    lax.fori_loop(0, chunks, shift_step, 0, unroll=True)
    ds_ref[prefix_rows:all_rows] = (p_own * (dp_ref[prefix_rows:all_rows] - centre)).astype(jnp.bfloat16)
    pb_ref[prefix_rows:all_rows] = p_own.astype(jnp.bfloat16)
    ds_all = ds_ref[...]
    dk_all = jnp.dot(ds_all, q_rows, preferred_element_type=jnp.float32) * scaling
    dv_all = jnp.dot(pb_ref[...], g_rows, preferred_element_type=jnp.float32)
    for i, r in enumerate(part_refs):
        r[0, :, cols] = dk_all[i * piece_len:(i + 1) * piece_len].astype(jnp.bfloat16)
        r[1, :, cols] = dv_all[i * piece_len:(i + 1) * piece_len].astype(jnp.bfloat16)
    dkown_ref[...] = dk_all[prefix_rows:all_rows].astype(jnp.bfloat16)
    dvown_ref[...] = dv_all[prefix_rows:all_rows].astype(jnp.bfloat16)
    dq_rows = lax.dot_general(ds_all, k_all, contract_major, preferred_element_type=jnp.float32) * scaling
    for h in range(group_size):
        dq_ref[:, h * HEAD_DIM:(h + 1) * HEAD_DIM] = dq_rows[h * resp_len:(h + 1) * resp_len].astype(jnp.bfloat16)


def split_words(value):
    high = value.astype(jnp.bfloat16)
    rest = value - high.astype(jnp.float32)
    middle = rest.astype(jnp.bfloat16)
    low = (rest - middle.astype(jnp.float32)).astype(jnp.bfloat16)
    return jnp.stack([high, middle, low])


def shifted(value, shift, n):
    return lax.ppermute(value, "resp", [(i, (i + shift) % n) for i in range(n)])


def on_device(
    queries,
    cotangent,
    resp_keys,
    resp_values,
    prefix_keys,
    prefix_values,
    counts,
    lengths,
    policy_likelihood,
    reference_likelihood,
):
    n = lax.axis_size("resp")
    slot_count = queries.shape[1]
    assert slot_count == 1
    resp_len = queries.shape[2]
    piece_len = prefix_keys.shape[1]
    live_count = counts[0]
    count_real = live_count.astype(jnp.float32)
    slot_ids = lax.axis_index("resp") * slot_count + jnp.arange(slot_count, dtype=jnp.int32)
    live_slots = slot_ids < live_count
    margin = policy_likelihood[0] - reference_likelihood[0]
    weight = jnp.where(live_slots, 2.0 * jax.nn.sigmoid(loss_beta * margin) / count_real, 0.0)
    loss_terms = jnp.where(live_slots, 2.0 / loss_beta * jax.nn.softplus(loss_beta * margin), 0.0)
    own_term = jnp.sum(loss_terms)
    word_rows = jnp.zeros((16, prefix_keys.shape[2]), jnp.bfloat16)
    word_rows = word_rows.at[0, 0:3].set(split_words(own_term))
    local_kv = jnp.concatenate([prefix_keys[0], prefix_values[0], word_rows], axis=0)
    if n == 4:
        from_left = shifted(local_kv, 1, n)
        pieces = [local_kv, from_left, shifted(local_kv, -1, n), shifted(from_left, 1, n)]
    else:
        pieces = [local_kv] + [shifted(local_kv, k, n) for k in range(1, n)]
    scalars = jnp.stack([weight[0], lengths[0][0].astype(jnp.float32), own_term, count_real])
    group_width = (HEADS // KV_HEADS) * HEAD_DIM
    group_rows = (HEADS // KV_HEADS) * resp_len
    all_rows = n * piece_len + resp_len
    piece_block = pl.BlockSpec(memory_space=pltpu.VMEM)
    part_block = pl.BlockSpec(memory_space=pltpu.VMEM)
    results = pl.pallas_call(
        functools.partial(attention_kernel, n),
        grid=(KV_HEADS,),
        in_specs=[
            pl.BlockSpec(memory_space=pltpu.SMEM),
            pl.BlockSpec(memory_space=pltpu.VMEM),
            pl.BlockSpec(memory_space=pltpu.VMEM),
            pl.BlockSpec((resp_len, HEAD_DIM), lambda g: (0, g)),
            pl.BlockSpec((resp_len, HEAD_DIM), lambda g: (0, g)),
        ]
        + [piece_block] * n,
        out_specs=[
            pl.BlockSpec((resp_len, group_width), lambda g: (0, g)),
            pl.BlockSpec((resp_len, HEAD_DIM), lambda g: (0, g)),
            pl.BlockSpec((resp_len, HEAD_DIM), lambda g: (0, g)),
        ]
        + [part_block] * n
        + [pl.BlockSpec(memory_space=pltpu.SMEM)],
        out_shape=[
            jax.ShapeDtypeStruct(queries.shape[2:], jnp.bfloat16),
            jax.ShapeDtypeStruct(resp_keys.shape[2:], jnp.bfloat16),
            jax.ShapeDtypeStruct(resp_values.shape[2:], jnp.bfloat16),
        ]
        + [jax.ShapeDtypeStruct((2,) + prefix_keys.shape[1:], jnp.bfloat16) for _ in range(n)]
        + [jax.ShapeDtypeStruct((1,), jnp.float32)],
        scratch_shapes=[pltpu.VMEM((all_rows, group_rows), jnp.float32) for _ in range(3)]
        + [pltpu.VMEM((all_rows, group_rows), jnp.bfloat16) for _ in range(2)],
        compiler_params=pltpu.CompilerParams(vmem_limit_bytes=48 * 1024 * 1024),
    )(scalars, queries[0, 0], cotangent[0, 0], resp_keys[0, 0], resp_values[0, 0], *pieces)
    grad_q, grad_k, grad_v = results[:3]
    parts = results[3:-1]
    forget_loss = results[-1]
    if n == 4:
        relayed = shifted(parts[3], -1, n)
        merged = (parts[1].astype(jnp.float32) + relayed.astype(jnp.float32)).astype(jnp.bfloat16)
        returned = [parts[0], shifted(parts[2], 1, n), shifted(merged, -1, n)]
    else:
        returned = [parts[0]] + [shifted(parts[k], -k, n) for k in range(1, n)]
    early_sum = lax.optimization_barrier(sum(r.astype(jnp.float32) for r in returned[:-1]))
    summed = early_sum + returned[-1].astype(jnp.float32)
    summed_keys = summed[0].astype(jnp.bfloat16)
    summed_values = summed[1].astype(jnp.bfloat16)
    return (
        grad_q[None, None],
        grad_k[None, None],
        grad_v[None, None],
        summed_keys[None],
        summed_values[None],
        forget_loss,
    )


def solution(mesh):
    placed = (
        P(("groups", "prompt"), "resp", None, None),
        P(("groups", "prompt"), "resp", None, None),
        P(("groups", "prompt"), "resp", None, None),
        P(("groups", "prompt"), "resp", None, None),
        P(("groups", "prompt"), "resp", None),
        P(("groups", "prompt"), "resp", None),
        P(("groups", "prompt")),
        P(("groups", "prompt"), "resp"),
        P(("groups", "prompt"), "resp"),
        P(("groups", "prompt"), "resp"),
    )
    return jax.shard_map(
        on_device,
        mesh=mesh,
        in_specs=placed,
        out_specs=(
            P(("groups", "prompt"), "resp", None, None),
            P(("groups", "prompt"), "resp", None, None),
            P(("groups", "prompt"), "resp", None, None),
            P(("groups", "prompt"), "resp", None),
            P(("groups", "prompt"), "resp", None),
            P(("groups", "prompt")),
        ),
        check_vma=False,
    )
```

```python
import functools
import math

import jax
import jax.numpy as jnp
from jax import lax
from jax.experimental import pallas as pl
from jax.experimental.pallas import tpu as pltpu
from jax.sharding import PartitionSpec as P

HEADS = 64
KV_HEADS = 4
HEAD_DIM = 128


loss_beta = 0.5
masked_score = -1e30


def attention_kernel(n_pieces, scalar_ref, q_ref, cot_ref, kown_ref, vown_ref, *rest):
    piece_refs = rest[:n_pieces]
    dq_ref, dkown_ref, dvown_ref = rest[n_pieces:n_pieces + 3]
    part_refs = rest[n_pieces + 3:2 * n_pieces + 3]
    loss_ref = rest[2 * n_pieces + 3]
    s_ref, dp_ref, e_ref, ds_ref, pb_ref = rest[2 * n_pieces + 4:]
    group_size = HEADS // KV_HEADS
    resp_len = q_ref.shape[0]
    piece_len = part_refs[0].shape[1]
    prefix_rows = n_pieces * piece_len
    all_rows = prefix_rows + resp_len
    scaling = 1.0 / math.sqrt(HEAD_DIM)
    exp_scale = scaling * math.log2(math.e)
    rows = group_size * resp_len
    chunk = 32
    chunks = prefix_rows // chunk
    token = lax.broadcasted_iota(jnp.int32, (resp_len, 1), 0).astype(jnp.float32)
    factor = jnp.where(token < scalar_ref[1], scalar_ref[0], 0.0)

    @pl.when(pl.program_id(0) == 0)
    def _():
        term_total = scalar_ref[2]
        for r in piece_refs[1:]:
            term_total = term_total + jnp.sum(r[2 * piece_len:2 * piece_len + 8, :].astype(jnp.float32))
        loss_ref[0] = term_total / scalar_ref[3]

    contract_minor = (((1,), (1,)), ((), ()))
    contract_major = (((0,), (0,)), ((), ()))
    q_all = q_ref[...]
    g_all = cot_ref[...]
    q_rows = jnp.concatenate([q_all[:, h * HEAD_DIM:(h + 1) * HEAD_DIM] for h in range(group_size)], axis=0)
    g_rows = jnp.concatenate([g_all[:, h * HEAD_DIM:(h + 1) * HEAD_DIM] for h in range(group_size)], axis=0)
    cols = pl.ds(pl.multiple_of(pl.program_id(0) * HEAD_DIM, HEAD_DIM), HEAD_DIM)
    k_all = jnp.concatenate([r[:piece_len, cols] for r in piece_refs] + [kown_ref[...]], axis=0)
    v_all = jnp.concatenate([r[piece_len:2 * piece_len, cols] for r in piece_refs] + [vown_ref[...]], axis=0)
    s_ref[...] = lax.dot_general(k_all, q_rows, contract_minor, preferred_element_type=jnp.float32)
    dp_ref[...] = lax.dot_general(v_all, g_rows, contract_minor, preferred_element_type=jnp.float32)
    own_pos = lax.broadcasted_iota(jnp.int32, (resp_len, rows), 0)
    token_of_col = lax.broadcasted_iota(jnp.int32, (resp_len, rows), 1) % resp_len
    s_own = jnp.where(token_of_col >= own_pos, s_ref[prefix_rows:all_rows], masked_score)

    def block(c):
        return pl.ds(pl.multiple_of(c * chunk, chunk), chunk)

    def max_step(c, running):
        return jnp.maximum(running, s_ref[block(c)])

    running = lax.fori_loop(0, chunks, max_step, jnp.full((chunk, rows), masked_score, jnp.float32), unroll=True)
    peak = jnp.maximum(jnp.max(running, axis=0, keepdims=True), jnp.max(s_own, axis=0, keepdims=True))

    def exp_step(c, running):
        e = jnp.exp2((s_ref[block(c)] - peak) * exp_scale)
        e_ref[block(c)] = e
        return running + e

    running = lax.fori_loop(0, chunks, exp_step, jnp.zeros((chunk, rows), jnp.float32), unroll=True)
    e_own = jnp.exp2((s_own - peak) * exp_scale)
    e_ref[prefix_rows:all_rows] = e_own
    total = jnp.sum(running, axis=0, keepdims=True) + jnp.sum(e_own, axis=0, keepdims=True)
    inv_total = 1.0 / total

    def centre_step(c, running):
        return running + (e_ref[block(c)] * inv_total) * dp_ref[block(c)]

    running = lax.fori_loop(0, chunks, centre_step, jnp.zeros((chunk, rows), jnp.float32), unroll=True)
    p_own = e_own * inv_total
    centre = jnp.sum(running, axis=0, keepdims=True) + jnp.sum(
        p_own * dp_ref[prefix_rows:all_rows], axis=0, keepdims=True
    )

    def shift_step(c, carry):
        p = e_ref[block(c)] * inv_total
        ds_ref[block(c)] = (p * (dp_ref[block(c)] - centre)).astype(jnp.bfloat16)
        pb_ref[block(c)] = p.astype(jnp.bfloat16)
        return carry

    lax.fori_loop(0, chunks, shift_step, 0, unroll=True)
    ds_ref[prefix_rows:all_rows] = (p_own * (dp_ref[prefix_rows:all_rows] - centre)).astype(jnp.bfloat16)
    pb_ref[prefix_rows:all_rows] = p_own.astype(jnp.bfloat16)
    ds_all = ds_ref[...]
    dk_all = jnp.dot(ds_all, q_rows, preferred_element_type=jnp.float32) * scaling
    dv_all = jnp.dot(pb_ref[...], g_rows, preferred_element_type=jnp.float32)
    for i, r in enumerate(part_refs):
        r[0, :, cols] = dk_all[i * piece_len:(i + 1) * piece_len].astype(jnp.bfloat16)
        r[1, :, cols] = dv_all[i * piece_len:(i + 1) * piece_len].astype(jnp.bfloat16)
    dkown_ref[...] = dk_all[prefix_rows:all_rows].astype(jnp.bfloat16)
    dvown_ref[...] = dv_all[prefix_rows:all_rows].astype(jnp.bfloat16)
    dq_rows = lax.dot_general(ds_all, k_all, contract_major, preferred_element_type=jnp.float32) * scaling
    for h in range(group_size):
        dq_ref[:, h * HEAD_DIM:(h + 1) * HEAD_DIM] = dq_rows[h * resp_len:(h + 1) * resp_len].astype(jnp.bfloat16)


def split_words(value):
    high = value.astype(jnp.bfloat16)
    rest = value - high.astype(jnp.float32)
    middle = rest.astype(jnp.bfloat16)
    low = (rest - middle.astype(jnp.float32)).astype(jnp.bfloat16)
    return jnp.stack([high, middle, low])


def shifted(value, shift, n):
    return lax.ppermute(value, "resp", [(i, (i + shift) % n) for i in range(n)])


def on_device(
    queries,
    cotangent,
    resp_keys,
    resp_values,
    prefix_keys,
    prefix_values,
    counts,
    lengths,
    policy_likelihood,
    reference_likelihood,
):
    n = lax.axis_size("resp")
    slot_count = queries.shape[1]
    assert slot_count == 1
    resp_len = queries.shape[2]
    piece_len = prefix_keys.shape[1]
    live_count = counts[0]
    count_real = live_count.astype(jnp.float32)
    slot_ids = lax.axis_index("resp") * slot_count + jnp.arange(slot_count, dtype=jnp.int32)
    live_slots = slot_ids < live_count
    margin = policy_likelihood[0] - reference_likelihood[0]
    weight = jnp.where(live_slots, 2.0 * jax.nn.sigmoid(loss_beta * margin) / count_real, 0.0)
    loss_terms = jnp.where(live_slots, 2.0 / loss_beta * jax.nn.softplus(loss_beta * margin), 0.0)
    own_term = jnp.sum(loss_terms)
    word_rows = jnp.zeros((16, prefix_keys.shape[2]), jnp.bfloat16)
    word_rows = word_rows.at[0, 0:3].set(split_words(own_term))
    local_kv = jnp.concatenate([prefix_keys[0], prefix_values[0], word_rows], axis=0)
    if n == 4:
        from_left = shifted(local_kv, 1, n)
        pieces = [local_kv, from_left, shifted(local_kv, -1, n), shifted(from_left, 1, n)]
    else:
        pieces = [local_kv] + [shifted(local_kv, k, n) for k in range(1, n)]
    scalars = jnp.stack([weight[0], lengths[0][0].astype(jnp.float32), own_term, count_real])
    positions = jnp.arange(resp_len, dtype=jnp.int32)
    factor = jnp.where(positions < lengths[0][0], weight[0], 0.0)
    grad_out = (cotangent[0, 0].astype(jnp.float32) * factor[:, None]).astype(jnp.bfloat16)
    group_width = (HEADS // KV_HEADS) * HEAD_DIM
    group_rows = (HEADS // KV_HEADS) * resp_len
    all_rows = n * piece_len + resp_len
    piece_block = pl.BlockSpec(memory_space=pltpu.VMEM)
    part_block = pl.BlockSpec(memory_space=pltpu.VMEM)
    results = pl.pallas_call(
        functools.partial(attention_kernel, n),
        grid=(KV_HEADS,),
        in_specs=[
            pl.BlockSpec(memory_space=pltpu.SMEM),
            pl.BlockSpec((resp_len, group_width), lambda g: (0, g)),
            pl.BlockSpec((resp_len, group_width), lambda g: (0, g)),
            pl.BlockSpec((resp_len, HEAD_DIM), lambda g: (0, g)),
            pl.BlockSpec((resp_len, HEAD_DIM), lambda g: (0, g)),
        ]
        + [piece_block] * n,
        out_specs=[
            pl.BlockSpec((resp_len, group_width), lambda g: (0, g)),
            pl.BlockSpec((resp_len, HEAD_DIM), lambda g: (0, g)),
            pl.BlockSpec((resp_len, HEAD_DIM), lambda g: (0, g)),
        ]
        + [part_block] * n
        + [pl.BlockSpec(memory_space=pltpu.SMEM)],
        out_shape=[
            jax.ShapeDtypeStruct(queries.shape[2:], jnp.bfloat16),
            jax.ShapeDtypeStruct(resp_keys.shape[2:], jnp.bfloat16),
            jax.ShapeDtypeStruct(resp_values.shape[2:], jnp.bfloat16),
        ]
        + [jax.ShapeDtypeStruct((2,) + prefix_keys.shape[1:], jnp.bfloat16) for _ in range(n)]
        + [jax.ShapeDtypeStruct((1,), jnp.float32)],
        scratch_shapes=[pltpu.VMEM((all_rows, group_rows), jnp.float32) for _ in range(3)]
        + [pltpu.VMEM((all_rows, group_rows), jnp.bfloat16) for _ in range(2)],
        compiler_params=pltpu.CompilerParams(vmem_limit_bytes=48 * 1024 * 1024),
    )(scalars, queries[0, 0], grad_out, resp_keys[0, 0], resp_values[0, 0], *pieces)
    grad_q, grad_k, grad_v = results[:3]
    parts = results[3:-1]
    forget_loss = results[-1]
    if n == 4:
        relayed = shifted(parts[3], -1, n)
        merged = (parts[1].astype(jnp.float32) + relayed.astype(jnp.float32)).astype(jnp.bfloat16)
        returned = [parts[0], shifted(parts[2], 1, n), shifted(merged, -1, n)]
    else:
        returned = [parts[0]] + [shifted(parts[k], -k, n) for k in range(1, n)]
    summed_keys = sum(r[0].astype(jnp.float32) for r in returned).astype(jnp.bfloat16)
    summed_values = sum(r[1].astype(jnp.float32) for r in returned).astype(jnp.bfloat16)
    return (
        grad_q[None, None],
        grad_k[None, None],
        grad_v[None, None],
        summed_keys[None],
        summed_values[None],
        forget_loss,
    )


def solution(mesh):
    placed = (
        P(("groups", "prompt"), "resp", None, None),
        P(("groups", "prompt"), "resp", None, None),
        P(("groups", "prompt"), "resp", None, None),
        P(("groups", "prompt"), "resp", None, None),
        P(("groups", "prompt"), "resp", None),
        P(("groups", "prompt"), "resp", None),
        P(("groups", "prompt")),
        P(("groups", "prompt"), "resp"),
        P(("groups", "prompt"), "resp"),
        P(("groups", "prompt"), "resp"),
    )
    return jax.shard_map(
        on_device,
        mesh=mesh,
        in_specs=placed,
        out_specs=(
            P(("groups", "prompt"), "resp", None, None),
            P(("groups", "prompt"), "resp", None, None),
            P(("groups", "prompt"), "resp", None, None),
            P(("groups", "prompt"), "resp", None),
            P(("groups", "prompt"), "resp", None),
            P(("groups", "prompt")),
        ),
        check_vma=False,
    )
```
